128 devices in a mesh: seq: 64 (over x, y, z_lo, core), row: 2 (over z_hi).
Axes of the slice: x: 4, y: 4, z: 4 (z_hi: 2, z_lo: 2; z = z_hi * 2 + z_lo), core: 2. Of those that a mesh axis runs over, the one named last changes fastest.
Arguments:
- queries: bfloat16 [2, 64, 128, 3072], P(None, 'seq', 'row'), may hold values from -9 to 9
- keys: bfloat16 [2, 64, 128, 512], P(None, 'seq', 'row'), may hold values from -9 to 9
- values: bfloat16 [2, 64, 128, 512], P(None, 'seq', 'row'), may hold values from -6 to 6
- gain: float32 [128], replicated, may hold values from 0.1 to 1.9
Outputs:
- attended: bfloat16 [2, 64, 128, 3072], P(None, 'seq', 'row')
The draws below stay inside these ranges and needn't reach their ends.
All inputs are finite; a program needn't handle non-finite values.
Results may differ from the reference program's by a relative error of at most 0.017.
Values may be sent and summed in bfloat16 or wider, within the bound.
No kernel may reach another device: no remote copies, remote signals or barrier semaphores. Data moves between devices by JAX's collectives and lax.ppermute only.
A program may use at most 128 MiB of HBM per device.

```python
import math
import jax
import jax.numpy as jnp
from jax import lax

BLOCK = 128
KV_HEADS = 4
GROUP = 6
HEAD_DIM = 128
HEADS = 24
BLOCKS = 128
SEQ_LEN = 16384


def to_layout_drawn(sequence_rows):
    width_now = sequence_rows.shape[-1]
    blocked = sequence_rows.reshape(BLOCKS, BLOCK, width_now)
    half_count = BLOCKS // 2
    return jnp.stack([blocked[:half_count], blocked[half_count:][::-1]], axis=0)


def draw_queries(key, part):
    width_now = HEADS * HEAD_DIM
    drawn = jnp.clip(jax.random.normal(jax.random.fold_in(key, 11), (SEQ_LEN, width_now), jnp.float32), -6.0, 6.0)
    return to_layout_drawn(drawn).astype(jnp.bfloat16)


def draw_keys(key, part):
    width_now = KV_HEADS * HEAD_DIM
    drawn = jnp.clip(jax.random.normal(jax.random.fold_in(key, 13), (SEQ_LEN, width_now), jnp.float32), -6.0, 6.0)
    return to_layout_drawn(drawn).astype(jnp.bfloat16)


def block_scale(own_key, extent, split, low, top_value):
    loudness = 1.0
    for axis_at, shards_of in split:
        steps = jax.random.uniform(jax.random.fold_in(jax.random.fold_in(own_key, 6), axis_at), (shards_of,), jnp.float32, low / len(split), top_value / len(split))
        loudness = loudness * jnp.repeat(jnp.exp(steps), extent[axis_at] // shards_of).reshape((-1,) + (1,) * (len(extent) - 1 - axis_at))
    return loudness


def normal_values(stream_key, extent, scale, reach, shards=(), kind=jnp.bfloat16):
    factor_of = block_scale(stream_key, extent, shards, -0.22, 0.18) if shards else 1.0
    array = jax.random.normal(stream_key, extent, jnp.float32) * scale * factor_of
    return jnp.minimum(jnp.maximum(array, -reach), reach).astype(kind)


def setup_inputs(seed: int = 0) -> dict:
    key_list = jax.random.split(jax.random.key(seed), 5)
    queries = draw_queries(jax.random.fold_in(key_list[4], 71), 0)
    keys = draw_keys(jax.random.fold_in(key_list[4], 71), 0)
    values = normal_values(key_list[2], (2, BLOCKS // 2, BLOCK, KV_HEADS * HEAD_DIM), 1.0, 6.0, ((1, 64), (2, 2)))
    gain = jnp.clip(1.0 + 0.18 * jax.random.normal(key_list[3], (HEAD_DIM,), jnp.float32), 0.1, 1.9)
    return dict(queries=queries, keys=keys, values=values, gain=gain)


def to_sequence(arranged):
    return jnp.concatenate([arranged[0], arranged[1][::-1]], axis=0)

def to_layout(blocked):
    half_count = BLOCKS // 2
    return jnp.stack([blocked[:half_count], blocked[half_count:][::-1]], axis=0)

def reference(queries, keys, values, gain):
    query_blocks = to_sequence(queries).reshape(BLOCKS, BLOCK, KV_HEADS, GROUP, HEAD_DIM)
    key_all = to_sequence(keys).reshape(SEQ_LEN, KV_HEADS, HEAD_DIM).astype(jnp.float32)
    value_all = to_sequence(values).reshape(SEQ_LEN, KV_HEADS, HEAD_DIM).astype(jnp.float32)
    key_block_ids = jnp.arange(SEQ_LEN, dtype=jnp.int32) // BLOCK
    scale_factor = 1.0 / math.sqrt(HEAD_DIM)
    gain_f = gain.astype(jnp.float32)

    def one_block(operands):
        query_block, block_index = operands
        scores = jnp.einsum('qgjd,kgd->qgjk', query_block.astype(jnp.float32), key_all)
        scores = scores * scale_factor
        visible = key_block_ids <= block_index
        scores = jnp.where(visible, scores, -jnp.inf)
        largest = lax.optimization_barrier(jnp.max(scores, axis=-1, keepdims=True))
        raw_weights = jnp.exp(scores - largest)
        totals = lax.optimization_barrier(jnp.sum(raw_weights, axis=-1))
        weights = lax.optimization_barrier(raw_weights.astype(jnp.bfloat16))
        mixed = jnp.einsum('qgjk,kgd->qgjd', weights.astype(jnp.float32), value_all) / totals[..., None]
        spread = jnp.sqrt(lax.optimization_barrier(jnp.mean(mixed * mixed, axis=-1, keepdims=True)) + 1e-06)
        return (mixed / spread * gain_f).astype(jnp.bfloat16)
    produced = lax.map(one_block, (query_blocks, jnp.arange(BLOCKS, dtype=jnp.int32)))
    return to_layout(produced.reshape(BLOCKS, BLOCK, HEADS * HEAD_DIM))
```

```python
import functools
import math

import jax
import jax.numpy as jnp
from jax import lax
from jax.experimental import pallas as pl
from jax.experimental.pallas import tpu as pltpu
from jax.sharding import PartitionSpec as P

KV_HEADS = 4
GROUP = 6
HEAD_DIM = 128
TILE_BLOCKS = 8

lowest_score = -1e30


def attend_kernel(bounds_ref, q_ref, k_ref, v_ref, gain_ref, *rest, rows, finalize, carry_in):
    if carry_in:
        m_in, l_in, acc_in = rest[:3]
        rest = rest[3:]
    if finalize:
        o_ref = rest[0]
        rest = rest[1:]
    else:
        m_out, l_out, acc_out = rest[:3]
        rest = rest[3:]
    q_sc, m_sc, l_sc, acc_sc = rest

    t = pl.program_id(1)
    last = pl.num_programs(1) - 1
    lo = bounds_ref[0]
    hi = bounds_ref[1]
    tile = lo // TILE_BLOCKS + t
    block_rows = k_ref.shape[1]

    @pl.when(t == 0)
    def _init():
        q_sc[...] = jnp.concatenate(
            [q_ref[:, j * HEAD_DIM:(j + 1) * HEAD_DIM] for j in range(GROUP)], axis=0
        )
        if carry_in:
            m_sc[...] = m_in[0]
            l_sc[...] = l_in[0]
            acc_sc[...] = acc_in[0]
        else:
            m_sc[...] = jnp.full(m_sc.shape, lowest_score, jnp.float32)
            l_sc[...] = jnp.zeros(l_sc.shape, jnp.float32)
            acc_sc[...] = jnp.zeros(acc_sc.shape, jnp.float32)

    @pl.when(tile <= hi // TILE_BLOCKS)
    def _step():
        keys = k_ref[...].reshape(TILE_BLOCKS * block_rows, HEAD_DIM)
        vals = v_ref[...].reshape(TILE_BLOCKS * block_rows, HEAD_DIM)
        scores = lax.dot_general(
            q_sc[...], keys, (((1,), (1,)), ((), ())), preferred_element_type=jnp.float32
        )
        scores = scores * (1.0 / math.sqrt(HEAD_DIM))
        key_block = tile * TILE_BLOCKS + lax.broadcasted_iota(jnp.int32, scores.shape, 1) // block_rows
        visible = (key_block >= lo) & (key_block <= hi)
        scores = jnp.where(visible, scores, -jnp.inf)
        running_max = m_sc[...]
        new_max = jnp.maximum(running_max, jnp.max(scores, axis=1, keepdims=True))
        raw_weights = jnp.exp(scores - new_max)
        factor = jnp.exp(running_max - new_max)
        l_sc[...] = l_sc[...] * factor + jnp.sum(raw_weights, axis=1, keepdims=True)
        acc_sc[...] = acc_sc[...] * factor + jnp.dot(
            raw_weights.astype(jnp.bfloat16), vals, preferred_element_type=jnp.float32
        )
        m_sc[...] = new_max

    @pl.when(t == last)
    def _done():
        if finalize:
            mixed = acc_sc[...] / l_sc[...]
            spread = jnp.sqrt(jnp.mean(mixed * mixed, axis=1, keepdims=True) + 1e-06)
            normed = (mixed / spread * gain_ref[...]).astype(o_ref.dtype)
            for j in range(GROUP):
                o_ref[:, j * HEAD_DIM:(j + 1) * HEAD_DIM] = normed[j * rows:(j + 1) * rows]
        else:
            m_out[0] = m_sc[...]
            l_out[0] = l_sc[...]
            acc_out[0] = acc_sc[...]


def attend(bounds, q, kv, gain, state=None, finalize=True):
    rows = q.shape[0]
    n_blocks, block_rows, _ = kv.shape
    n_tiles = n_blocks // TILE_BLOCKS
    qrows = rows * GROUP

    def tile_of(t, b):
        return jnp.minimum(b[0] // TILE_BLOCKS + t, b[1] // TILE_BLOCKS)

    in_specs = [
        pl.BlockSpec((rows, GROUP * HEAD_DIM), lambda g, t, b: (0, g)),
        pl.BlockSpec((TILE_BLOCKS, block_rows, HEAD_DIM), lambda g, t, b: (tile_of(t, b), 0, g)),
        pl.BlockSpec(
            (TILE_BLOCKS, block_rows, HEAD_DIM), lambda g, t, b: (tile_of(t, b), 0, KV_HEADS + g)
        ),
        pl.BlockSpec((1, HEAD_DIM), lambda g, t, b: (0, 0)),
    ]
    operands = [q, kv, kv, gain.reshape(1, HEAD_DIM)]
    state_specs = [
        pl.BlockSpec((1, qrows, 1), lambda g, t, b: (g, 0, 0)),
        pl.BlockSpec((1, qrows, 1), lambda g, t, b: (g, 0, 0)),
        pl.BlockSpec((1, qrows, HEAD_DIM), lambda g, t, b: (g, 0, 0)),
    ]
    state_shapes = [
        jax.ShapeDtypeStruct((KV_HEADS, qrows, 1), jnp.float32),
        jax.ShapeDtypeStruct((KV_HEADS, qrows, 1), jnp.float32),
        jax.ShapeDtypeStruct((KV_HEADS, qrows, HEAD_DIM), jnp.float32),
    ]
    if state is not None:
        in_specs += state_specs
        operands += list(state)
    if finalize:
        out_specs = pl.BlockSpec((rows, GROUP * HEAD_DIM), lambda g, t, b: (0, g))
        out_shape = jax.ShapeDtypeStruct((rows, KV_HEADS * GROUP * HEAD_DIM), jnp.bfloat16)
    else:
        out_specs = state_specs
        out_shape = state_shapes
    kernel = functools.partial(
        attend_kernel, rows=rows, finalize=finalize, carry_in=state is not None
    )
    tile_flops = 4 * qrows * TILE_BLOCKS * block_rows * HEAD_DIM
    cost = pl.CostEstimate(
        flops=KV_HEADS * n_tiles * tile_flops,
        transcendentals=KV_HEADS * n_tiles * qrows * TILE_BLOCKS * block_rows,
        bytes_accessed=kv.size * 2 + q.size * 4,
    )
    return pl.pallas_call(
        kernel,
        grid_spec=pltpu.PrefetchScalarGridSpec(
            num_scalar_prefetch=1,
            grid=(KV_HEADS, n_tiles),
            in_specs=in_specs,
            out_specs=out_specs,
            scratch_shapes=[
                pltpu.VMEM((qrows, HEAD_DIM), jnp.bfloat16),
                pltpu.VMEM((qrows, 1), jnp.float32),
                pltpu.VMEM((qrows, 1), jnp.float32),
                pltpu.VMEM((qrows, HEAD_DIM), jnp.float32),
            ],
        ),
        out_shape=out_shape,
        compiler_params=pltpu.CompilerParams(
            dimension_semantics=("arbitrary", "arbitrary"),
        ),
        cost_estimate=cost,
    )(bounds, *operands)


def per_device(queries, keys, values, gain):
    seq_index = lax.axis_index("seq")
    last_index = lax.axis_size("seq") - 1
    own_rows = queries.shape[2]
    pair = jnp.concatenate([keys, values], axis=-1)
    pair = lax.all_gather(pair, "row", axis=2, tiled=True)
    low_blocks = lax.all_gather(pair[0, 0], "seq", axis=0, tiled=True)
    low_blocks = low_blocks.reshape(-1, pair.shape[2], pair.shape[3])
    high_blocks = lax.all_gather(pair[1, 0], "seq", axis=0, tiled=True)
    high_blocks = high_blocks.reshape(-1, pair.shape[2], pair.shape[3])
    zero = jnp.int32(0)
    top = jnp.int32(last_index)
    early = attend(jnp.stack([zero, seq_index]), queries[0, 0], low_blocks, gain)
    state = attend(
        jnp.stack([zero, top]), queries[1, 0], low_blocks, gain, finalize=False
    )
    late = attend(jnp.stack([seq_index, top]), queries[1, 0], high_blocks, gain, state=state)
    return jnp.stack([early, late]).reshape(2, 1, own_rows, KV_HEADS * GROUP * HEAD_DIM)


def solution(mesh):
    return jax.shard_map(
        per_device,
        mesh=mesh,
        in_specs=(
            P(None, "seq", "row", None),
            P(None, "seq", "row", None),
            P(None, "seq", "row", None),
            P(),
        ),
        out_specs=P(None, "seq", "row", None),
        check_vma=False,
    )
```

```python
import functools
import math

import jax
import jax.numpy as jnp
from jax import lax
from jax.experimental import pallas as pl
from jax.experimental.pallas import tpu as pltpu
from jax.sharding import PartitionSpec as P

KV_HEADS = 4
GROUP = 6
HEAD_DIM = 128
TILE_KEYS = 1024

lowest_score = -1e30


def attend_kernel(bounds_ref, q_ref, k_ref, v_ref, *rest, carry_in):
    if carry_in:
        m_in, l_in, acc_in = rest[:3]
        rest = rest[3:]
    m_out, l_out, acc_out = rest[:3]
    q_sc, m_sc, l_sc, acc_sc = rest[3:]

    t = pl.program_id(1)
    last = pl.num_programs(1) - 1
    tile_blocks, block_rows, _ = k_ref.shape
    lo = bounds_ref[0]
    hi = bounds_ref[1]
    tile = lo // tile_blocks + t
    first_block = tile * tile_blocks

    @pl.when(t == 0)
    def _init():
        q_sc[...] = jnp.concatenate(
            [q_ref[:, j * HEAD_DIM:(j + 1) * HEAD_DIM] for j in range(GROUP)], axis=0
        )
        if carry_in:
            m_sc[...] = m_in[0]
            l_sc[...] = l_in[0]
            acc_sc[...] = acc_in[0]
        else:
            m_sc[...] = jnp.full(m_sc.shape, lowest_score, jnp.float32)
            l_sc[...] = jnp.zeros(l_sc.shape, jnp.float32)
            acc_sc[...] = jnp.zeros(acc_sc.shape, jnp.float32)

    def step(masked):
        keys = k_ref[...].reshape(tile_blocks * block_rows, HEAD_DIM)
        vals = v_ref[...].reshape(tile_blocks * block_rows, HEAD_DIM)
        scores = lax.dot_general(
            q_sc[...], keys, (((1,), (1,)), ((), ())), preferred_element_type=jnp.float32
        )
        scores = scores * (1.0 / math.sqrt(HEAD_DIM))
        if masked:
            key_block = first_block + lax.broadcasted_iota(jnp.int32, scores.shape, 1) // block_rows
            visible = (key_block >= lo) & (key_block <= hi)
            scores = jnp.where(visible, scores, -jnp.inf)
        running_max = m_sc[...]
        new_max = jnp.maximum(running_max, jnp.max(scores, axis=1, keepdims=True))
        raw_weights = jnp.exp(scores - new_max)
        factor = jnp.exp(running_max - new_max)
        l_sc[...] = l_sc[...] * factor + jnp.sum(raw_weights, axis=1, keepdims=True)
        acc_sc[...] = acc_sc[...] * factor + jnp.dot(
            raw_weights.astype(jnp.bfloat16), vals, preferred_element_type=jnp.float32
        )
        m_sc[...] = new_max

    active = tile <= hi // tile_blocks
    edge = (first_block < lo) | (first_block + tile_blocks - 1 > hi)

    @pl.when(active & edge)
    def _edge_step():
        step(True)

    @pl.when(active & jnp.logical_not(edge))
    def _inner_step():
        step(False)

    @pl.when(t == last)
    def _done():
        m_out[0] = m_sc[...]
        l_out[0] = l_sc[...]
        acc_out[0] = acc_sc[...]


def attend(bounds, q, kv, state=None):
    rows = q.shape[0]
    n_blocks, block_rows, _ = kv.shape
    tile_blocks = TILE_KEYS // block_rows
    n_tiles = n_blocks // tile_blocks
    qrows = rows * GROUP

    def tile_of(t, b):
        return jnp.minimum(b[0] // tile_blocks + t, b[1] // tile_blocks)

    in_specs = [
        pl.BlockSpec((rows, GROUP * HEAD_DIM), lambda g, t, b: (0, g)),
        pl.BlockSpec((tile_blocks, block_rows, HEAD_DIM), lambda g, t, b: (tile_of(t, b), 0, g)),
        pl.BlockSpec(
            (tile_blocks, block_rows, HEAD_DIM), lambda g, t, b: (tile_of(t, b), 0, KV_HEADS + g)
        ),
    ]
    operands = [q, kv, kv]
    state_specs = [
        pl.BlockSpec((1, qrows, 1), lambda g, t, b: (g, 0, 0)),
        pl.BlockSpec((1, qrows, 1), lambda g, t, b: (g, 0, 0)),
        pl.BlockSpec((1, qrows, HEAD_DIM), lambda g, t, b: (g, 0, 0)),
    ]
    state_shapes = [
        jax.ShapeDtypeStruct((KV_HEADS, qrows, 1), jnp.float32),
        jax.ShapeDtypeStruct((KV_HEADS, qrows, 1), jnp.float32),
        jax.ShapeDtypeStruct((KV_HEADS, qrows, HEAD_DIM), jnp.float32),
    ]
    if state is not None:
        in_specs += state_specs
        operands += list(state)
    kernel = functools.partial(attend_kernel, carry_in=state is not None)
    tile_flops = 4 * qrows * TILE_KEYS * HEAD_DIM
    cost = pl.CostEstimate(
        flops=KV_HEADS * n_tiles * tile_flops,
        transcendentals=KV_HEADS * n_tiles * qrows * TILE_KEYS,
        bytes_accessed=kv.size * 2 + q.size * 2 + KV_HEADS * qrows * HEAD_DIM * 8,
    )
    return pl.pallas_call(
        kernel,
        grid_spec=pltpu.PrefetchScalarGridSpec(
            num_scalar_prefetch=1,
            grid=(KV_HEADS, n_tiles),
            in_specs=in_specs,
            out_specs=state_specs,
            scratch_shapes=[
                pltpu.VMEM((qrows, HEAD_DIM), jnp.bfloat16),
                pltpu.VMEM((qrows, 1), jnp.float32),
                pltpu.VMEM((qrows, 1), jnp.float32),
                pltpu.VMEM((qrows, HEAD_DIM), jnp.float32),
            ],
        ),
        out_shape=state_shapes,
        compiler_params=pltpu.CompilerParams(
            dimension_semantics=("arbitrary", "arbitrary"),
        ),
        cost_estimate=cost,
    )(bounds, *operands)


def split_halves(state, own_rows):
    mine, theirs = [], []
    for part in state:
        shaped = part.reshape(KV_HEADS, GROUP, 2, own_rows, part.shape[-1])
        mine.append(shaped[:, :, 0])
        theirs.append(shaped[:, :, 1])
    return mine, theirs


def finish(mine, theirs, gain):
    own_max, own_sum, own_acc = mine
    far_max, far_sum, far_acc = theirs
    top = jnp.maximum(own_max, far_max)
    own_factor = jnp.exp(own_max - top)
    far_factor = jnp.exp(far_max - top)
    total = own_sum * own_factor + far_sum * far_factor
    acc = own_acc * own_factor + far_acc * far_factor
    mixed = acc / total
    spread = jnp.sqrt(jnp.mean(mixed * mixed, axis=-1, keepdims=True) + 1e-06)
    normed = (mixed / spread * gain).astype(jnp.bfloat16)
    rows = normed.shape[2]
    return normed.transpose(2, 0, 1, 3).reshape(rows, KV_HEADS * GROUP * HEAD_DIM)


def per_device(queries, keys, values, gain):
    seq_index = lax.axis_index("seq")
    last_index = lax.axis_size("seq") - 1
    own_rows = queries.shape[2]
    swap = [(0, 1), (1, 0)]
    partner_queries = lax.ppermute(queries, "row", swap)
    both_queries = jnp.concatenate([queries, partner_queries], axis=2)
    pair = jnp.concatenate([keys, values], axis=-1)
    low_blocks = lax.all_gather(pair[0, 0], "seq", axis=0, tiled=True)
    low_blocks = low_blocks.reshape(-1, own_rows, pair.shape[3])
    high_blocks = lax.all_gather(pair[1, 0], "seq", axis=0, tiled=True)
    high_blocks = high_blocks.reshape(-1, own_rows, pair.shape[3])
    zero = jnp.int32(0)
    top = jnp.int32(last_index)

    early = attend(jnp.stack([zero, seq_index]), both_queries[0, 0], low_blocks)
    early_mine, early_theirs = split_halves(early, own_rows)
    early_back = [lax.ppermute(x, "row", swap) for x in early_theirs]

    state = attend(jnp.stack([zero, top]), both_queries[1, 0], low_blocks)
    late = attend(jnp.stack([seq_index, top]), both_queries[1, 0], high_blocks, state=state)
    late_mine, late_theirs = split_halves(late, own_rows)
    late_back = [lax.ppermute(x, "row", swap) for x in late_theirs]

    early_out = finish(early_mine, early_back, gain)
    late_out = finish(late_mine, late_back, gain)
    return jnp.stack([early_out, late_out]).reshape(2, 1, own_rows, KV_HEADS * GROUP * HEAD_DIM)


def solution(mesh):
    return jax.shard_map(
        per_device,
        mesh=mesh,
        in_specs=(
            P(None, "seq", "row", None),
            P(None, "seq", "row", None),
            P(None, "seq", "row", None),
            P(),
        ),
        out_specs=P(None, "seq", "row", None),
        check_vma=False,
    )
```

```python
import functools
import math

import jax
import jax.numpy as jnp
from jax import lax
from jax.experimental import pallas as pl
from jax.experimental.pallas import tpu as pltpu
from jax.sharding import PartitionSpec as P

KV_HEADS = 4
GROUP = 6
HEAD_DIM = 128
TILE_KEYS = 1024

lowest_score = -1e30


def attend_kernel(bounds_ref, q_ref, k_ref, v_ref, *rest, carry_in):
    if carry_in:
        m_in, l_in, acc_in = rest[:3]
        rest = rest[3:]
    m_out, l_out, acc_out = rest[:3]
    q_sc, m_sc, l_sc, acc_sc = rest[3:]

    t = pl.program_id(1)
    last = pl.num_programs(1) - 1
    tile_blocks, block_rows, _ = k_ref.shape
    lo = bounds_ref[0]
    hi = bounds_ref[1]
    tile = lo // tile_blocks + t
    first_block = tile * tile_blocks

    @pl.when(t == 0)
    def _init():
        q_sc[...] = jnp.concatenate(
            [q_ref[:, j * HEAD_DIM:(j + 1) * HEAD_DIM] for j in range(GROUP)], axis=0
        )
        if carry_in:
            m_sc[...] = m_in[0]
            l_sc[...] = l_in[0]
            acc_sc[...] = acc_in[0]
        else:
            m_sc[...] = jnp.full(m_sc.shape, lowest_score, jnp.float32)
            l_sc[...] = jnp.zeros(l_sc.shape, jnp.float32)
            acc_sc[...] = jnp.zeros(acc_sc.shape, jnp.float32)

    def step(masked):
        keys = k_ref[...].reshape(tile_blocks * block_rows, HEAD_DIM)
        vals = v_ref[...].reshape(tile_blocks * block_rows, HEAD_DIM)
        half = q_sc.shape[0] // 2
        for part in range(2):
            rows_here = pl.ds(part * half, half)
            half_step(masked, keys, vals, rows_here)

    def half_step(masked, keys, vals, rows_here):
        scores = lax.dot_general(
            q_sc[rows_here], keys, (((1,), (1,)), ((), ())), preferred_element_type=jnp.float32
        )
        scores = scores * (1.0 / math.sqrt(HEAD_DIM))
        if masked:
            key_block = first_block + lax.broadcasted_iota(jnp.int32, scores.shape, 1) // block_rows
            visible = (key_block >= lo) & (key_block <= hi)
            scores = jnp.where(visible, scores, -jnp.inf)
        running_max = m_sc[rows_here]
        new_max = jnp.maximum(running_max, jnp.max(scores, axis=1, keepdims=True))
        raw_weights = jnp.exp(scores - new_max)
        factor = jnp.exp(running_max - new_max)
        l_sc[rows_here] = l_sc[rows_here] * factor + jnp.sum(raw_weights, axis=1, keepdims=True)
        acc_sc[rows_here] = acc_sc[rows_here] * factor + jnp.dot(
            raw_weights.astype(jnp.bfloat16), vals, preferred_element_type=jnp.float32
        )
        m_sc[rows_here] = new_max

    active = tile <= hi // tile_blocks
    edge = (first_block < lo) | (first_block + tile_blocks - 1 > hi)

    @pl.when(active & edge)
    def _edge_step():
        step(True)

    @pl.when(active & jnp.logical_not(edge))
    def _inner_step():
        step(False)

    @pl.when(t == last)
    def _done():
        m_out[0] = m_sc[...]
        l_out[0] = l_sc[...]
        acc_out[0] = acc_sc[...]


def attend(bounds, q, kv, half, state=None):
    rows = q.shape[0]
    _, n_blocks, block_rows, _ = kv.shape
    tile_blocks = TILE_KEYS // block_rows
    n_tiles = n_blocks // tile_blocks
    qrows = rows * GROUP

    def tile_of(t, b):
        return jnp.minimum(b[0] // tile_blocks + t, b[1] // tile_blocks)

    in_specs = [
        pl.BlockSpec((rows, GROUP * HEAD_DIM), lambda g, t, b: (0, g)),
        pl.BlockSpec(
            (None, tile_blocks, block_rows, HEAD_DIM),
            lambda g, t, b: (half, tile_of(t, b), 0, g),
        ),
        pl.BlockSpec(
            (None, tile_blocks, block_rows, HEAD_DIM),
            lambda g, t, b: (half, tile_of(t, b), 0, KV_HEADS + g),
        ),
    ]
    operands = [q, kv, kv]
    state_specs = [
        pl.BlockSpec((1, qrows, 1), lambda g, t, b: (g, 0, 0)),
        pl.BlockSpec((1, qrows, 1), lambda g, t, b: (g, 0, 0)),
        pl.BlockSpec((1, qrows, HEAD_DIM), lambda g, t, b: (g, 0, 0)),
    ]
    state_shapes = [
        jax.ShapeDtypeStruct((KV_HEADS, qrows, 1), jnp.float32),
        jax.ShapeDtypeStruct((KV_HEADS, qrows, 1), jnp.float32),
        jax.ShapeDtypeStruct((KV_HEADS, qrows, HEAD_DIM), jnp.float32),
    ]
    if state is not None:
        in_specs += state_specs
        operands += list(state)
    kernel = functools.partial(attend_kernel, carry_in=state is not None)
    tile_flops = 4 * qrows * TILE_KEYS * HEAD_DIM
    cost = pl.CostEstimate(
        flops=KV_HEADS * n_tiles * tile_flops,
        transcendentals=KV_HEADS * n_tiles * qrows * TILE_KEYS,
        bytes_accessed=kv.size + q.size * 2 + KV_HEADS * qrows * HEAD_DIM * 8,
    )
    return pl.pallas_call(
        kernel,
        grid_spec=pltpu.PrefetchScalarGridSpec(
            num_scalar_prefetch=1,
            grid=(KV_HEADS, n_tiles),
            in_specs=in_specs,
            out_specs=state_specs,
            scratch_shapes=[
                pltpu.VMEM((qrows, HEAD_DIM), jnp.bfloat16),
                pltpu.VMEM((qrows, 1), jnp.float32),
                pltpu.VMEM((qrows, 1), jnp.float32),
                pltpu.VMEM((qrows, HEAD_DIM), jnp.float32),
            ],
        ),
        out_shape=state_shapes,
        compiler_params=pltpu.CompilerParams(
            dimension_semantics=("arbitrary", "arbitrary"),
        ),
        cost_estimate=cost,
    )(bounds, *operands)


def split_halves(state, own_rows):
    mine, theirs = [], []
    for part in state:
        shaped = part.reshape(KV_HEADS, GROUP, 2, own_rows, part.shape[-1])
        mine.append(shaped[:, :, 0])
        theirs.append(shaped[:, :, 1])
    return mine, theirs


def finish(mine, theirs, gain):
    own_max, own_sum, own_acc = mine
    far_max, far_sum, far_acc = theirs
    top = jnp.maximum(own_max, far_max)
    own_factor = jnp.exp(own_max - top)
    far_factor = jnp.exp(far_max - top)
    total = own_sum * own_factor + far_sum * far_factor
    acc = own_acc * own_factor + far_acc * far_factor
    mixed = acc / total
    spread = jnp.sqrt(jnp.mean(mixed * mixed, axis=-1, keepdims=True) + 1e-06)
    normed = (mixed / spread * gain).astype(jnp.bfloat16)
    rows = normed.shape[2]
    return normed.transpose(2, 0, 1, 3).reshape(rows, KV_HEADS * GROUP * HEAD_DIM)


def per_device(queries, keys, values, gain):
    seq_index = lax.axis_index("seq")
    last_index = lax.axis_size("seq") - 1
    own_rows = queries.shape[2]
    swap = [(0, 1), (1, 0)]
    partner_queries = lax.ppermute(queries, "row", swap)
    both_queries = jnp.concatenate([queries, partner_queries], axis=2)
    pair = jnp.concatenate([keys, values], axis=-1)
    blocks = lax.all_gather(pair[:, 0], "seq", axis=1, tiled=False)
    zero = jnp.int32(0)
    top = jnp.int32(last_index)

    early = attend(jnp.stack([zero, seq_index]), both_queries[0, 0], blocks, 0)
    early_mine, early_theirs = split_halves(early, own_rows)
    early_back = [lax.ppermute(x, "row", swap) for x in early_theirs]

    state = attend(jnp.stack([zero, top]), both_queries[1, 0], blocks, 0)
    late = attend(jnp.stack([seq_index, top]), both_queries[1, 0], blocks, 1, state=state)
    late_mine, late_theirs = split_halves(late, own_rows)
    late_back = [lax.ppermute(x, "row", swap) for x in late_theirs]

    early_out = finish(early_mine, early_back, gain)
    late_out = finish(late_mine, late_back, gain)
    return jnp.stack([early_out, late_out]).reshape(2, 1, own_rows, KV_HEADS * GROUP * HEAD_DIM)


def solution(mesh):
    return jax.shard_map(
        per_device,
        mesh=mesh,
        in_specs=(
            P(None, "seq", "row", None),
            P(None, "seq", "row", None),
            P(None, "seq", "row", None),
            P(),
        ),
        out_specs=P(None, "seq", "row", None),
        check_vma=False,
    )
```

```python
import functools
import math

import jax
import jax.numpy as jnp
from jax import lax
from jax.experimental import pallas as pl
from jax.experimental.pallas import tpu as pltpu
from jax.sharding import PartitionSpec as P

KV_HEADS = 4
GROUP = 6
HEAD_DIM = 128
TILE_KEYS = 1024

lowest_score = -1e30


def attend_kernel(bounds_ref, q_ref, k_ref, v_ref, *rest, carry_in):
    if carry_in:
        m_in, l_in, acc_in = rest[:3]
        rest = rest[3:]
    m_out, l_out, acc_out = rest[:3]
    q_sc, m_sc, l_sc, acc_sc = rest[3:]

    t = pl.program_id(1)
    last = pl.num_programs(1) - 1
    tile_blocks, block_rows, _ = k_ref.shape
    lo = bounds_ref[0]
    hi = bounds_ref[1]
    tile = lo // tile_blocks + t
    first_block = tile * tile_blocks

    @pl.when(t == 0)
    def _init():
        q_sc[...] = jnp.concatenate(
            [q_ref[:, j * HEAD_DIM:(j + 1) * HEAD_DIM] for j in range(GROUP)], axis=0
        )
        if carry_in:
            m_sc[...] = m_in[0]
            l_sc[...] = l_in[0]
            acc_sc[...] = acc_in[0]
        else:
            m_sc[...] = jnp.full(m_sc.shape, lowest_score, jnp.float32)
            l_sc[...] = jnp.zeros(l_sc.shape, jnp.float32)
            acc_sc[...] = jnp.zeros(acc_sc.shape, jnp.float32)

    def step(masked):
        keys = k_ref[...].reshape(tile_blocks * block_rows, HEAD_DIM)
        vals = v_ref[...].reshape(tile_blocks * block_rows, HEAD_DIM)
        half = q_sc.shape[0] // 2
        bias = None
        if masked:
            key_block = first_block + lax.broadcasted_iota(
                jnp.int32, (1, tile_blocks * block_rows), 1
            ) // block_rows
            visible = (key_block >= lo) & (key_block <= hi)
            bias = jnp.where(visible, 0.0, -jnp.inf).astype(jnp.float32)
        for part in range(2):
            rows_here = pl.ds(part * half, half)
            half_step(bias, keys, vals, rows_here)

    def half_step(bias, keys, vals, rows_here):
        scores = lax.dot_general(
            q_sc[rows_here], keys, (((1,), (1,)), ((), ())), preferred_element_type=jnp.float32
        )
        scores = scores * (1.0 / math.sqrt(HEAD_DIM))
        if bias is not None:
            scores = scores + bias
        running_max = m_sc[rows_here]
        new_max = jnp.maximum(running_max, jnp.max(scores, axis=1, keepdims=True))
        raw_weights = jnp.exp(scores - new_max)
        factor = jnp.exp(running_max - new_max)
        l_sc[rows_here] = l_sc[rows_here] * factor + jnp.sum(raw_weights, axis=1, keepdims=True)
        acc_sc[rows_here] = acc_sc[rows_here] * factor + jnp.dot(
            raw_weights.astype(jnp.bfloat16), vals, preferred_element_type=jnp.float32
        )
        m_sc[rows_here] = new_max

    active = tile <= hi // tile_blocks
    edge = (first_block < lo) | (first_block + tile_blocks - 1 > hi)

    @pl.when(active & edge)
    def _edge_step():
        step(True)

    @pl.when(active & jnp.logical_not(edge))
    def _inner_step():
        step(False)

    @pl.when(t == last)
    def _done():
        m_out[0] = m_sc[...]
        l_out[0] = l_sc[...]
        acc_out[0] = acc_sc[...]


def attend(bounds, q, kv, half, state=None):
    rows = q.shape[0]
    _, n_blocks, block_rows, _ = kv.shape
    tile_blocks = TILE_KEYS // block_rows
    n_tiles = n_blocks // tile_blocks
    qrows = rows * GROUP

    def tile_of(t, b):
        return jnp.minimum(b[0] // tile_blocks + t, b[1] // tile_blocks)

    in_specs = [
        pl.BlockSpec((rows, GROUP * HEAD_DIM), lambda g, t, b: (0, g)),
        pl.BlockSpec(
            (None, tile_blocks, block_rows, HEAD_DIM),
            lambda g, t, b: (half, tile_of(t, b), 0, g),
        ),
        pl.BlockSpec(
            (None, tile_blocks, block_rows, HEAD_DIM),
            lambda g, t, b: (half, tile_of(t, b), 0, KV_HEADS + g),
        ),
    ]
    operands = [q, kv, kv]
    state_specs = [
        pl.BlockSpec((1, qrows, 1), lambda g, t, b: (g, 0, 0)),
        pl.BlockSpec((1, qrows, 1), lambda g, t, b: (g, 0, 0)),
        pl.BlockSpec((1, qrows, HEAD_DIM), lambda g, t, b: (g, 0, 0)),
    ]
    state_shapes = [
        jax.ShapeDtypeStruct((KV_HEADS, qrows, 1), jnp.float32),
        jax.ShapeDtypeStruct((KV_HEADS, qrows, 1), jnp.float32),
        jax.ShapeDtypeStruct((KV_HEADS, qrows, HEAD_DIM), jnp.float32),
    ]
    if state is not None:
        in_specs += state_specs
        operands += list(state)
    kernel = functools.partial(attend_kernel, carry_in=state is not None)
    tile_flops = 4 * qrows * TILE_KEYS * HEAD_DIM
    cost = pl.CostEstimate(
        flops=KV_HEADS * n_tiles * tile_flops,
        transcendentals=KV_HEADS * n_tiles * qrows * TILE_KEYS,
        bytes_accessed=kv.size + q.size * 2 + KV_HEADS * qrows * HEAD_DIM * 8,
    )
    return pl.pallas_call(
        kernel,
        grid_spec=pltpu.PrefetchScalarGridSpec(
            num_scalar_prefetch=1,
            grid=(KV_HEADS, n_tiles),
            in_specs=in_specs,
            out_specs=state_specs,
            scratch_shapes=[
                pltpu.VMEM((qrows, HEAD_DIM), jnp.bfloat16),
                pltpu.VMEM((qrows, 1), jnp.float32),
                pltpu.VMEM((qrows, 1), jnp.float32),
                pltpu.VMEM((qrows, HEAD_DIM), jnp.float32),
            ],
        ),
        out_shape=state_shapes,
        compiler_params=pltpu.CompilerParams(
            dimension_semantics=("arbitrary", "arbitrary"),
        ),
        cost_estimate=cost,
    )(bounds, *operands)


def split_halves(state, own_rows):
    mine, theirs = [], []
    for part in state:
        shaped = part.reshape(KV_HEADS, GROUP, 2, own_rows, part.shape[-1])
        mine.append(shaped[:, :, 0])
        theirs.append(shaped[:, :, 1])
    return mine, theirs


def finish(mine, theirs, gain):
    own_max, own_sum, own_acc = mine
    far_max, far_sum, far_acc = theirs
    top = jnp.maximum(own_max, far_max)
    own_factor = jnp.exp(own_max - top)
    far_factor = jnp.exp(far_max - top)
    total = own_sum * own_factor + far_sum * far_factor
    acc = own_acc * own_factor + far_acc * far_factor
    mixed = acc / total
    spread = jnp.sqrt(jnp.mean(mixed * mixed, axis=-1, keepdims=True) + 1e-06)
    normed = (mixed / spread * gain).astype(jnp.bfloat16)
    rows = normed.shape[2]
    return normed.transpose(2, 0, 1, 3).reshape(rows, KV_HEADS * GROUP * HEAD_DIM)


def per_device(queries, keys, values, gain):
    seq_index = lax.axis_index("seq")
    last_index = lax.axis_size("seq") - 1
    own_rows = queries.shape[2]
    swap = [(0, 1), (1, 0)]
    partner_queries = lax.ppermute(queries, "row", swap)
    both_queries = jnp.concatenate([queries, partner_queries], axis=2)
    pair = jnp.concatenate([keys, values], axis=-1)
    blocks = lax.all_gather(pair[:, 0], "seq", axis=1, tiled=False)
    zero = jnp.int32(0)
    top = jnp.int32(last_index)

    early = attend(jnp.stack([zero, seq_index]), both_queries[0, 0], blocks, 0)
    early_mine, early_theirs = split_halves(early, own_rows)
    early_back = [lax.ppermute(x, "row", swap) for x in early_theirs]

    state = attend(jnp.stack([zero, top]), both_queries[1, 0], blocks, 0)
    late = attend(jnp.stack([seq_index, top]), both_queries[1, 0], blocks, 1, state=state)
    late_mine, late_theirs = split_halves(late, own_rows)
    late_back = [lax.ppermute(x, "row", swap) for x in late_theirs]

    early_out = finish(early_mine, early_back, gain)
    late_out = finish(late_mine, late_back, gain)
    return jnp.stack([early_out, late_out]).reshape(2, 1, own_rows, KV_HEADS * GROUP * HEAD_DIM)


def solution(mesh):
    return jax.shard_map(
        per_device,
        mesh=mesh,
        in_specs=(
            P(None, "seq", "row", None),
            P(None, "seq", "row", None),
            P(None, "seq", "row", None),
            P(),
        ),
        out_specs=P(None, "seq", "row", None),
        check_vma=False,
    )
```

```python
import functools
import math

import jax
import jax.numpy as jnp
from jax import lax
from jax.experimental import pallas as pl
from jax.experimental.pallas import tpu as pltpu
from jax.sharding import PartitionSpec as P

KV_HEADS = 4
GROUP = 6
HEAD_DIM = 128
TILE_KEYS = 1024

lowest_score = -1e30
EXP2_SCALE = math.log2(math.e) / math.sqrt(HEAD_DIM)


def attend_kernel(bounds_ref, q_ref, k_ref, v_ref, *rest, carry_in):
    if carry_in:
        m_in, l_in, acc_in = rest[:3]
        rest = rest[3:]
    m_out, l_out, acc_out = rest[:3]
    q_sc, m_sc, l_sc, acc_sc, vals_sc = rest[3:]

    t = pl.program_id(1)
    last = pl.num_programs(1) - 1
    tile_blocks, block_rows, _ = k_ref.shape
    lo = bounds_ref[0]
    hi = bounds_ref[1]
    tile = lo // tile_blocks + t
    first_block = tile * tile_blocks

    @pl.when(t == 0)
    def _init():
        vals_sc[:, HEAD_DIM:] = jnp.ones((vals_sc.shape[0], HEAD_DIM), jnp.bfloat16)
        q_sc[...] = jnp.concatenate(
            [q_ref[:, j * HEAD_DIM:(j + 1) * HEAD_DIM] for j in range(GROUP)], axis=0
        )
        if carry_in:
            m_sc[...] = m_in[0]
            l_sc[...] = l_in[0]
            acc_sc[...] = acc_in[0]
        else:
            m_sc[...] = jnp.full(m_sc.shape, lowest_score, jnp.float32)
            l_sc[...] = jnp.zeros(l_sc.shape, jnp.float32)
            acc_sc[...] = jnp.zeros(acc_sc.shape, jnp.float32)

    def step(masked):
        keys = k_ref[...].reshape(tile_blocks * block_rows, HEAD_DIM)
        vals_sc[:, :HEAD_DIM] = v_ref[...].reshape(tile_blocks * block_rows, HEAD_DIM)
        vals = vals_sc[...]
        half = q_sc.shape[0] // 2
        bias = None
        if masked:
            key_block = first_block + lax.broadcasted_iota(
                jnp.int32, (1, tile_blocks * block_rows), 1
            ) // block_rows
            visible = (key_block >= lo) & (key_block <= hi)
            bias = jnp.where(visible, 0.0, -jnp.inf).astype(jnp.float32)
        for part in range(2):
            rows_here = pl.ds(part * half, half)
            half_step(bias, keys, vals, rows_here)

    def half_step(bias, keys, vals, rows_here):
        scores = lax.dot_general(
            q_sc[rows_here], keys, (((1,), (1,)), ((), ())), preferred_element_type=jnp.float32
        )
        if bias is not None:
            scores = scores + bias
        running_max = m_sc[rows_here]
        new_max = jnp.maximum(running_max, jnp.max(scores, axis=1, keepdims=True))
        raw_weights = jnp.exp2((scores - new_max) * EXP2_SCALE)
        factor = jnp.exp2((running_max - new_max) * EXP2_SCALE)
        mixed = jnp.dot(
            raw_weights.astype(jnp.bfloat16), vals, preferred_element_type=jnp.float32
        )
        l_sc[rows_here] = l_sc[rows_here] * factor + mixed[:, HEAD_DIM:HEAD_DIM + 1]
        acc_sc[rows_here] = acc_sc[rows_here] * factor + mixed[:, :HEAD_DIM]
        m_sc[rows_here] = new_max

    active = tile <= hi // tile_blocks
    edge = (first_block < lo) | (first_block + tile_blocks - 1 > hi)

    @pl.when(active & edge)
    def _edge_step():
        step(True)

    @pl.when(active & jnp.logical_not(edge))
    def _inner_step():
        step(False)

    @pl.when(t == last)
    def _done():
        m_out[0] = m_sc[...]
        l_out[0] = l_sc[...]
        acc_out[0] = acc_sc[...]


def attend(bounds, q, kv, half, state=None):
    rows = q.shape[0]
    _, n_blocks, block_rows, _ = kv.shape
    tile_blocks = TILE_KEYS // block_rows
    n_tiles = n_blocks // tile_blocks
    qrows = rows * GROUP

    def tile_of(t, b):
        return jnp.minimum(b[0] // tile_blocks + t, b[1] // tile_blocks)

    in_specs = [
        pl.BlockSpec((rows, GROUP * HEAD_DIM), lambda g, t, b: (0, g)),
        pl.BlockSpec(
            (None, tile_blocks, block_rows, HEAD_DIM),
            lambda g, t, b: (half, tile_of(t, b), 0, g),
        ),
        pl.BlockSpec(
            (None, tile_blocks, block_rows, HEAD_DIM),
            lambda g, t, b: (half, tile_of(t, b), 0, KV_HEADS + g),
        ),
    ]
    operands = [q, kv, kv]
    state_specs = [
        pl.BlockSpec((1, qrows, 1), lambda g, t, b: (g, 0, 0)),
        pl.BlockSpec((1, qrows, 1), lambda g, t, b: (g, 0, 0)),
        pl.BlockSpec((1, qrows, HEAD_DIM), lambda g, t, b: (g, 0, 0)),
    ]
    state_shapes = [
        jax.ShapeDtypeStruct((KV_HEADS, qrows, 1), jnp.float32),
        jax.ShapeDtypeStruct((KV_HEADS, qrows, 1), jnp.float32),
        jax.ShapeDtypeStruct((KV_HEADS, qrows, HEAD_DIM), jnp.float32),
    ]
    if state is not None:
        in_specs += state_specs
        operands += list(state)
    kernel = functools.partial(attend_kernel, carry_in=state is not None)
    tile_flops = 4 * qrows * TILE_KEYS * HEAD_DIM
    cost = pl.CostEstimate(
        flops=KV_HEADS * n_tiles * tile_flops,
        transcendentals=KV_HEADS * n_tiles * qrows * TILE_KEYS,
        bytes_accessed=kv.size + q.size * 2 + KV_HEADS * qrows * HEAD_DIM * 8,
    )
    return pl.pallas_call(
        kernel,
        grid_spec=pltpu.PrefetchScalarGridSpec(
            num_scalar_prefetch=1,
            grid=(KV_HEADS, n_tiles),
            in_specs=in_specs,
            out_specs=state_specs,
            scratch_shapes=[
                pltpu.VMEM((qrows, HEAD_DIM), jnp.bfloat16),
                pltpu.VMEM((qrows, 1), jnp.float32),
                pltpu.VMEM((qrows, 1), jnp.float32),
                pltpu.VMEM((qrows, HEAD_DIM), jnp.float32),
                pltpu.VMEM((TILE_KEYS, 2 * HEAD_DIM), jnp.bfloat16),
            ],
        ),
        out_shape=state_shapes,
        compiler_params=pltpu.CompilerParams(
            dimension_semantics=("arbitrary", "arbitrary"),
        ),
        cost_estimate=cost,
    )(bounds, *operands)


def split_halves(state, own_rows):
    mine, theirs = [], []
    for part in state:
        shaped = part.reshape(KV_HEADS, GROUP, 2, own_rows, part.shape[-1])
        mine.append(shaped[:, :, 0])
        theirs.append(shaped[:, :, 1])
    return mine, theirs


def finish(mine, theirs, gain):
    own_max, own_sum, own_acc = mine
    far_max, far_sum, far_acc = theirs
    top = jnp.maximum(own_max, far_max)
    own_factor = jnp.exp2((own_max - top) * EXP2_SCALE)
    far_factor = jnp.exp2((far_max - top) * EXP2_SCALE)
    total = own_sum * own_factor + far_sum * far_factor
    acc = own_acc * own_factor + far_acc * far_factor
    mixed = acc / total
    spread = jnp.sqrt(jnp.mean(mixed * mixed, axis=-1, keepdims=True) + 1e-06)
    normed = (mixed / spread * gain).astype(jnp.bfloat16)
    rows = normed.shape[2]
    return normed.transpose(2, 0, 1, 3).reshape(rows, KV_HEADS * GROUP * HEAD_DIM)


def per_device(queries, keys, values, gain):
    seq_index = lax.axis_index("seq")
    last_index = lax.axis_size("seq") - 1
    own_rows = queries.shape[2]
    swap = [(0, 1), (1, 0)]
    partner_queries = lax.ppermute(queries, "row", swap)
    both_queries = jnp.concatenate([queries, partner_queries], axis=2)
    pair = jnp.concatenate([keys, values], axis=-1)
    blocks = lax.all_gather(pair[:, 0], "seq", axis=1, tiled=False)
    zero = jnp.int32(0)
    top = jnp.int32(last_index)

    early = attend(jnp.stack([zero, seq_index]), both_queries[0, 0], blocks, 0)
    early_mine, early_theirs = split_halves(early, own_rows)
    early_back = [lax.ppermute(x, "row", swap) for x in early_theirs]

    state = attend(jnp.stack([zero, top]), both_queries[1, 0], blocks, 0)
    late = attend(jnp.stack([seq_index, top]), both_queries[1, 0], blocks, 1, state=state)
    late_mine, late_theirs = split_halves(late, own_rows)
    late_back = [lax.ppermute(x, "row", swap) for x in late_theirs]

    early_out = finish(early_mine, early_back, gain)
    late_out = finish(late_mine, late_back, gain)
    return jnp.stack([early_out, late_out]).reshape(2, 1, own_rows, KV_HEADS * GROUP * HEAD_DIM)


def solution(mesh):
    return jax.shard_map(
        per_device,
        mesh=mesh,
        in_specs=(
            P(None, "seq", "row", None),
            P(None, "seq", "row", None),
            P(None, "seq", "row", None),
            P(),
        ),
        out_specs=P(None, "seq", "row", None),
        check_vma=False,
    )
```

```python
import functools
import math

import jax
import jax.numpy as jnp
from jax import lax
from jax.experimental import pallas as pl
from jax.experimental.pallas import tpu as pltpu
from jax.sharding import Mesh, PartitionSpec as P

KV_HEADS = 4
GROUP = 6
HEAD_DIM = 128
TILE_KEYS = 1024

lowest_score = -1e30
EXP2_SCALE = math.log2(math.e) / math.sqrt(HEAD_DIM)


def attend_kernel(bounds_ref, q_ref, k_ref, v_ref, *rest, carry_in):
    if carry_in:
        m_in, l_in, acc_in = rest[:3]
        rest = rest[3:]
    m_out, l_out, acc_out = rest[:3]
    q_sc, m_sc, l_sc, acc_sc, vals_sc = rest[3:]

    t = pl.program_id(1)
    last = pl.num_programs(1) - 1
    tile_blocks, block_rows, _ = k_ref.shape
    lo = bounds_ref[0]
    hi = bounds_ref[1]
    tile = lo // tile_blocks + t
    first_block = tile * tile_blocks

    @pl.when(t == 0)
    def _init():
        vals_sc[:, HEAD_DIM:] = jnp.ones((vals_sc.shape[0], HEAD_DIM), jnp.bfloat16)
        q_sc[...] = jnp.concatenate(
            [q_ref[:, j * HEAD_DIM:(j + 1) * HEAD_DIM] for j in range(GROUP)], axis=0
        )
        if carry_in:
            m_sc[...] = m_in[0]
            l_sc[...] = l_in[0]
            acc_sc[...] = acc_in[0]
        else:
            m_sc[...] = jnp.full(m_sc.shape, lowest_score, jnp.float32)
            l_sc[...] = jnp.zeros(l_sc.shape, jnp.float32)
            acc_sc[...] = jnp.zeros(acc_sc.shape, jnp.float32)

    def step(masked):
        keys = k_ref[...].reshape(tile_blocks * block_rows, HEAD_DIM)
        vals_sc[:, :HEAD_DIM] = v_ref[...].reshape(tile_blocks * block_rows, HEAD_DIM)
        vals = vals_sc[...]
        half = q_sc.shape[0] // 2
        bias = None
        if masked:
            key_block = first_block + lax.broadcasted_iota(
                jnp.int32, (1, tile_blocks * block_rows), 1
            ) // block_rows
            visible = (key_block >= lo) & (key_block <= hi)
            bias = jnp.where(visible, 0.0, -jnp.inf).astype(jnp.float32)
        for part in range(2):
            rows_here = pl.ds(part * half, half)
            half_step(bias, keys, vals, rows_here)

    def half_step(bias, keys, vals, rows_here):
        scores = lax.dot_general(
            q_sc[rows_here], keys, (((1,), (1,)), ((), ())), preferred_element_type=jnp.float32
        )
        if bias is not None:
            scores = scores + bias
        running_max = m_sc[rows_here]
        new_max = jnp.maximum(running_max, jnp.max(scores, axis=1, keepdims=True))
        raw_weights = jnp.exp2((scores - new_max) * EXP2_SCALE)
        factor = jnp.exp2((running_max - new_max) * EXP2_SCALE)
        mixed = jnp.dot(
            raw_weights.astype(jnp.bfloat16), vals, preferred_element_type=jnp.float32
        )
        l_sc[rows_here] = l_sc[rows_here] * factor + mixed[:, HEAD_DIM:HEAD_DIM + 1]
        acc_sc[rows_here] = acc_sc[rows_here] * factor + mixed[:, :HEAD_DIM]
        m_sc[rows_here] = new_max

    active = tile <= hi // tile_blocks
    edge = (first_block < lo) | (first_block + tile_blocks - 1 > hi)

    @pl.when(active & edge)
    def _edge_step():
        step(True)

    @pl.when(active & jnp.logical_not(edge))
    def _inner_step():
        step(False)

    @pl.when(t == last)
    def _done():
        m_out[0] = m_sc[...]
        l_out[0] = l_sc[...]
        acc_out[0] = acc_sc[...]


def attend(bounds, q, kv, half, state=None):
    rows = q.shape[0]
    _, n_blocks, block_rows, _ = kv.shape
    tile_blocks = TILE_KEYS // block_rows
    n_tiles = n_blocks // tile_blocks
    qrows = rows * GROUP

    def tile_of(t, b):
        return jnp.minimum(b[0] // tile_blocks + t, b[1] // tile_blocks)

    in_specs = [
        pl.BlockSpec((rows, GROUP * HEAD_DIM), lambda g, t, b: (0, g)),
        pl.BlockSpec(
            (None, tile_blocks, block_rows, HEAD_DIM),
            lambda g, t, b: (half, tile_of(t, b), 0, g),
        ),
        pl.BlockSpec(
            (None, tile_blocks, block_rows, HEAD_DIM),
            lambda g, t, b: (half, tile_of(t, b), 0, KV_HEADS + g),
        ),
    ]
    operands = [q, kv, kv]
    state_specs = [
        pl.BlockSpec((1, qrows, 1), lambda g, t, b: (g, 0, 0)),
        pl.BlockSpec((1, qrows, 1), lambda g, t, b: (g, 0, 0)),
        pl.BlockSpec((1, qrows, HEAD_DIM), lambda g, t, b: (g, 0, 0)),
    ]
    state_shapes = [
        jax.ShapeDtypeStruct((KV_HEADS, qrows, 1), jnp.float32),
        jax.ShapeDtypeStruct((KV_HEADS, qrows, 1), jnp.float32),
        jax.ShapeDtypeStruct((KV_HEADS, qrows, HEAD_DIM), jnp.float32),
    ]
    if state is not None:
        in_specs += state_specs
        operands += list(state)
    kernel = functools.partial(attend_kernel, carry_in=state is not None)
    tile_flops = 4 * qrows * TILE_KEYS * HEAD_DIM
    cost = pl.CostEstimate(
        flops=KV_HEADS * n_tiles * tile_flops,
        transcendentals=KV_HEADS * n_tiles * qrows * TILE_KEYS,
        bytes_accessed=kv.size + q.size * 2 + KV_HEADS * qrows * HEAD_DIM * 8,
    )
    return pl.pallas_call(
        kernel,
        grid_spec=pltpu.PrefetchScalarGridSpec(
            num_scalar_prefetch=1,
            grid=(KV_HEADS, n_tiles),
            in_specs=in_specs,
            out_specs=state_specs,
            scratch_shapes=[
                pltpu.VMEM((qrows, HEAD_DIM), jnp.bfloat16),
                pltpu.VMEM((qrows, 1), jnp.float32),
                pltpu.VMEM((qrows, 1), jnp.float32),
                pltpu.VMEM((qrows, HEAD_DIM), jnp.float32),
                pltpu.VMEM((TILE_KEYS, 2 * HEAD_DIM), jnp.bfloat16),
            ],
        ),
        out_shape=state_shapes,
        compiler_params=pltpu.CompilerParams(
            dimension_semantics=("arbitrary", "arbitrary"),
        ),
        cost_estimate=cost,
    )(bounds, *operands)


def split_halves(state, own_rows):
    mine, theirs = [], []
    for part in state:
        shaped = part.reshape(KV_HEADS, GROUP, 2, own_rows, part.shape[-1])
        mine.append(shaped[:, :, 0])
        theirs.append(shaped[:, :, 1])
    return mine, theirs


def finish(mine, theirs, gain):
    own_max, own_sum, own_acc = mine
    far_max, far_sum, far_acc = theirs
    top = jnp.maximum(own_max, far_max)
    own_factor = jnp.exp2((own_max - top) * EXP2_SCALE)
    far_factor = jnp.exp2((far_max - top) * EXP2_SCALE)
    total = own_sum * own_factor + far_sum * far_factor
    acc = own_acc * own_factor + far_acc * far_factor
    mixed = acc / total
    spread = jnp.sqrt(jnp.mean(mixed * mixed, axis=-1, keepdims=True) + 1e-06)
    normed = (mixed / spread * gain).astype(jnp.bfloat16)
    rows = normed.shape[2]
    return normed.transpose(2, 0, 1, 3).reshape(rows, KV_HEADS * GROUP * HEAD_DIM)


def per_device(queries, keys, values, gain, outer, inner):
    seq_index = lax.axis_index("outer") * inner + lax.axis_index("inner")
    last_index = outer * inner - 1
    own_rows = queries.shape[2]
    swap = [(0, 1), (1, 0)]
    partner_queries = lax.ppermute(queries, "row", swap)
    both_queries = jnp.concatenate([queries, partner_queries], axis=2)
    pair = jnp.concatenate([keys, values], axis=-1)
    blocks = lax.all_gather(pair[:, 0], "outer", axis=1, tiled=False)
    blocks = lax.all_gather(blocks, "inner", axis=2, tiled=False)
    blocks = blocks.reshape(2, outer * inner, own_rows, pair.shape[3])
    zero = jnp.int32(0)
    top = jnp.int32(last_index)

    early = attend(jnp.stack([zero, seq_index]), both_queries[0, 0], blocks, 0)
    early_mine, early_theirs = split_halves(early, own_rows)
    early_back = [lax.ppermute(x, "row", swap) for x in early_theirs]

    state = attend(jnp.stack([zero, top]), both_queries[1, 0], blocks, 0)
    late = attend(jnp.stack([seq_index, top]), both_queries[1, 0], blocks, 1, state=state)
    late_mine, late_theirs = split_halves(late, own_rows)
    late_back = [lax.ppermute(x, "row", swap) for x in late_theirs]

    early_out = finish(early_mine, early_back, gain)
    late_out = finish(late_mine, late_back, gain)
    return jnp.stack([early_out, late_out]).reshape(2, 1, own_rows, KV_HEADS * GROUP * HEAD_DIM)


def solution(mesh):
    seq_count, row_count = mesh.devices.shape
    outer = math.gcd(seq_count, 4)
    inner = seq_count // outer
    split = Mesh(mesh.devices.reshape(outer, inner, row_count), ("outer", "inner", "row"))
    spec = P(None, ("outer", "inner"), "row", None)
    return jax.shard_map(
        functools.partial(per_device, outer=outer, inner=inner),
        mesh=split,
        in_specs=(spec, spec, spec, P()),
        out_specs=spec,
        check_vma=False,
    )
```

```python
import functools
import math

import jax
import jax.numpy as jnp
from jax import lax
from jax.experimental import pallas as pl
from jax.experimental.pallas import tpu as pltpu
from jax.sharding import Mesh, PartitionSpec as P

KV_HEADS = 4
GROUP = 6
HEAD_DIM = 128
TILE_KEYS = 1024

lowest_score = -1e30
EXP2_SCALE = math.log2(math.e) / math.sqrt(HEAD_DIM)


def attend_kernel(bounds_ref, q_ref, k_ref, v_ref, *rest, carry_in):
    if carry_in:
        m_in, l_in, acc_in = rest[:3]
        rest = rest[3:]
    m_out, l_out, acc_out = rest[:3]
    q_sc, m_sc, l_sc, acc_sc, vals_sc = rest[3:]

    t = pl.program_id(1)
    last = pl.num_programs(1) - 1
    tile_blocks, block_rows, _ = k_ref.shape
    lo = bounds_ref[0]
    hi = bounds_ref[1]
    tile = lo // tile_blocks + t
    first_block = tile * tile_blocks

    @pl.when(t == 0)
    def _init():
        vals_sc[:, HEAD_DIM:] = jnp.ones((vals_sc.shape[0], HEAD_DIM), jnp.bfloat16)
        q_sc[...] = jnp.concatenate(
            [q_ref[:, j * HEAD_DIM:(j + 1) * HEAD_DIM] for j in range(GROUP)], axis=0
        )
        if carry_in:
            m_sc[...] = m_in[0]
            l_sc[...] = l_in[0]
            acc_sc[...] = acc_in[0]
        else:
            m_sc[...] = jnp.full(m_sc.shape, lowest_score, jnp.float32)
            l_sc[...] = jnp.zeros(l_sc.shape, jnp.float32)
            acc_sc[...] = jnp.zeros(acc_sc.shape, jnp.float32)

    def step(masked):
        keys = k_ref[...].reshape(tile_blocks * block_rows, HEAD_DIM)
        vals_sc[:, :HEAD_DIM] = v_ref[...].reshape(tile_blocks * block_rows, HEAD_DIM)
        vals = vals_sc[...]
        half = q_sc.shape[0] // 2
        bias = None
        if masked:
            key_block = first_block + lax.broadcasted_iota(
                jnp.int32, (1, tile_blocks * block_rows), 1
            ) // block_rows
            visible = (key_block >= lo) & (key_block <= hi)
            bias = jnp.where(visible, 0.0, -jnp.inf).astype(jnp.float32)
        for part in range(2):
            rows_here = pl.ds(part * half, half)
            half_step(bias, keys, vals, rows_here)

    def half_step(bias, keys, vals, rows_here):
        scores = lax.dot_general(
            q_sc[rows_here], keys, (((1,), (1,)), ((), ())), preferred_element_type=jnp.float32
        )
        if bias is not None:
            scores = scores + bias
        running_max = m_sc[rows_here]
        new_max = jnp.maximum(running_max, jnp.max(scores, axis=1, keepdims=True))
        raw_weights = jnp.exp2((scores - new_max) * EXP2_SCALE)
        factor = jnp.exp2((running_max - new_max) * EXP2_SCALE)
        mixed = jnp.dot(
            raw_weights.astype(jnp.bfloat16), vals, preferred_element_type=jnp.float32
        )
        l_sc[rows_here] = l_sc[rows_here] * factor + mixed[:, HEAD_DIM:HEAD_DIM + 1]
        acc_sc[rows_here] = acc_sc[rows_here] * factor + mixed[:, :HEAD_DIM]
        m_sc[rows_here] = new_max

    active = tile <= hi // tile_blocks
    edge = (first_block < lo) | (first_block + tile_blocks - 1 > hi)

    @pl.when(active & edge)
    def _edge_step():
        step(True)

    @pl.when(active & jnp.logical_not(edge))
    def _inner_step():
        step(False)

    @pl.when(t == last)
    def _done():
        m_out[0] = m_sc[...]
        l_out[0] = l_sc[...]
        acc_out[0] = acc_sc[...]


def attend(bounds, q, kv, half, state=None):
    rows = q.shape[0]
    _, n_blocks, block_rows, _ = kv.shape
    tile_blocks = TILE_KEYS // block_rows
    n_tiles = n_blocks // tile_blocks
    qrows = rows * GROUP

    def tile_of(t, b):
        return jnp.minimum(b[0] // tile_blocks + t, b[1] // tile_blocks)

    in_specs = [
        pl.BlockSpec((rows, GROUP * HEAD_DIM), lambda g, t, b: (0, g)),
        pl.BlockSpec(
            (None, tile_blocks, block_rows, HEAD_DIM),
            lambda g, t, b: (half, tile_of(t, b), 0, g),
        ),
        pl.BlockSpec(
            (None, tile_blocks, block_rows, HEAD_DIM),
            lambda g, t, b: (half, tile_of(t, b), 0, KV_HEADS + g),
        ),
    ]
    operands = [q, kv, kv]
    state_specs = [
        pl.BlockSpec((1, qrows, 1), lambda g, t, b: (g, 0, 0)),
        pl.BlockSpec((1, qrows, 1), lambda g, t, b: (g, 0, 0)),
        pl.BlockSpec((1, qrows, HEAD_DIM), lambda g, t, b: (g, 0, 0)),
    ]
    state_shapes = [
        jax.ShapeDtypeStruct((KV_HEADS, qrows, 1), jnp.float32),
        jax.ShapeDtypeStruct((KV_HEADS, qrows, 1), jnp.float32),
        jax.ShapeDtypeStruct((KV_HEADS, qrows, HEAD_DIM), jnp.float32),
    ]
    if state is not None:
        in_specs += state_specs
        operands += list(state)
    kernel = functools.partial(attend_kernel, carry_in=state is not None)
    tile_flops = 4 * qrows * TILE_KEYS * HEAD_DIM
    cost = pl.CostEstimate(
        flops=KV_HEADS * n_tiles * tile_flops,
        transcendentals=KV_HEADS * n_tiles * qrows * TILE_KEYS,
        bytes_accessed=kv.size + q.size * 2 + KV_HEADS * qrows * HEAD_DIM * 8,
    )
    return pl.pallas_call(
        kernel,
        grid_spec=pltpu.PrefetchScalarGridSpec(
            num_scalar_prefetch=1,
            grid=(KV_HEADS, n_tiles),
            in_specs=in_specs,
            out_specs=state_specs,
            scratch_shapes=[
                pltpu.VMEM((qrows, HEAD_DIM), jnp.bfloat16),
                pltpu.VMEM((qrows, 1), jnp.float32),
                pltpu.VMEM((qrows, 1), jnp.float32),
                pltpu.VMEM((qrows, HEAD_DIM), jnp.float32),
                pltpu.VMEM((TILE_KEYS, 2 * HEAD_DIM), jnp.bfloat16),
            ],
        ),
        out_shape=state_shapes,
        compiler_params=pltpu.CompilerParams(
            dimension_semantics=("arbitrary", "arbitrary"),
        ),
        cost_estimate=cost,
    )(bounds, *operands)


def split_halves(state, own_rows):
    mine, theirs = [], []
    for part in state:
        shaped = part.reshape(KV_HEADS, GROUP, 2, own_rows, part.shape[-1])
        mine.append(shaped[:, :, 0])
        theirs.append(shaped[:, :, 1])
    return mine, theirs


def send_back(theirs, swap):
    run_max, run_sum, acc = theirs
    acc = lax.ppermute(acc.astype(jnp.bfloat16), "row", swap).astype(jnp.float32)
    return [lax.ppermute(run_max, "row", swap), lax.ppermute(run_sum, "row", swap), acc]


def finish(mine, theirs, gain):
    own_max, own_sum, own_acc = mine
    far_max, far_sum, far_acc = theirs
    top = jnp.maximum(own_max, far_max)
    own_factor = jnp.exp2((own_max - top) * EXP2_SCALE)
    far_factor = jnp.exp2((far_max - top) * EXP2_SCALE)
    total = own_sum * own_factor + far_sum * far_factor
    acc = own_acc * own_factor + far_acc * far_factor
    mixed = acc / total
    spread = jnp.sqrt(jnp.mean(mixed * mixed, axis=-1, keepdims=True) + 1e-06)
    normed = (mixed / spread * gain).astype(jnp.bfloat16)
    rows = normed.shape[2]
    return normed.transpose(2, 0, 1, 3).reshape(rows, KV_HEADS * GROUP * HEAD_DIM)


def per_device(queries, keys, values, gain, outer, inner):
    seq_index = lax.axis_index("outer") * inner + lax.axis_index("inner")
    last_index = outer * inner - 1
    own_rows = queries.shape[2]
    swap = [(0, 1), (1, 0)]
    partner_queries = lax.ppermute(queries, "row", swap)
    both_queries = jnp.concatenate([queries, partner_queries], axis=2)
    pair = jnp.concatenate([keys, values], axis=-1)
    blocks = lax.all_gather(pair[:, 0], "outer", axis=1, tiled=False)
    blocks = lax.all_gather(blocks, "inner", axis=2, tiled=False)
    blocks = blocks.reshape(2, outer * inner, own_rows, pair.shape[3])
    zero = jnp.int32(0)
    top = jnp.int32(last_index)

    early = attend(jnp.stack([zero, seq_index]), both_queries[0, 0], blocks, 0)
    early_mine, early_theirs = split_halves(early, own_rows)
    early_back = send_back(early_theirs, swap)

    state = attend(jnp.stack([zero, top]), both_queries[1, 0], blocks, 0)
    late = attend(jnp.stack([seq_index, top]), both_queries[1, 0], blocks, 1, state=state)
    late_mine, late_theirs = split_halves(late, own_rows)
    late_back = send_back(late_theirs, swap)

    early_out = finish(early_mine, early_back, gain)
    late_out = finish(late_mine, late_back, gain)
    return jnp.stack([early_out, late_out]).reshape(2, 1, own_rows, KV_HEADS * GROUP * HEAD_DIM)


def solution(mesh):
    seq_count, row_count = mesh.devices.shape
    outer = math.gcd(seq_count, 4)
    inner = seq_count // outer
    split = Mesh(mesh.devices.reshape(outer, inner, row_count), ("outer", "inner", "row"))
    spec = P(None, ("outer", "inner"), "row", None)
    return jax.shard_map(
        functools.partial(per_device, outer=outer, inner=inner),
        mesh=split,
        in_specs=(spec, spec, spec, P()),
        out_specs=spec,
        check_vma=False,
    )
```

```python
import functools
import math

import jax
import jax.numpy as jnp
from jax import lax
from jax.experimental import pallas as pl
from jax.experimental.pallas import tpu as pltpu
from jax.sharding import Mesh, PartitionSpec as P

KV_HEADS = 4
GROUP = 6
HEAD_DIM = 128
TILE_KEYS = 1024

lowest_score = -1e30
EXP2_SCALE = math.log2(math.e) / math.sqrt(HEAD_DIM)


def attend_kernel(bounds_ref, q_ref, k_ref, v_ref, *rest, carry_in):
    if carry_in:
        m_in, l_in, acc_in = rest[:3]
        rest = rest[3:]
    m_out, l_out, acc_out = rest[:3]
    q_sc, m_sc, l_sc, acc_sc, vals_sc = rest[3:]

    t = pl.program_id(1)
    last = pl.num_programs(1) - 1
    tile_blocks, block_rows, _ = k_ref.shape
    lo = bounds_ref[0]
    hi = bounds_ref[1]
    tile = lo // tile_blocks + t
    first_block = tile * tile_blocks

    @pl.when(t == 0)
    def _init():
        vals_sc[:, HEAD_DIM:] = jnp.ones((vals_sc.shape[0], HEAD_DIM), jnp.bfloat16)
        grouped = jnp.concatenate(
            [q_ref[:, j * HEAD_DIM:(j + 1) * HEAD_DIM] for j in range(GROUP)], axis=0
        )
        q_sc[...] = (grouped.astype(jnp.float32) * EXP2_SCALE).astype(q_sc.dtype)
        if carry_in:
            m_sc[...] = m_in[0]
            l_sc[...] = l_in[0]
            acc_sc[...] = acc_in[0]
        else:
            m_sc[...] = jnp.full(m_sc.shape, lowest_score, jnp.float32)
            l_sc[...] = jnp.zeros(l_sc.shape, jnp.float32)
            acc_sc[...] = jnp.zeros(acc_sc.shape, jnp.float32)

    def step(masked):
        keys = k_ref[...].reshape(tile_blocks * block_rows, HEAD_DIM)
        vals_sc[:, :HEAD_DIM] = v_ref[...].reshape(tile_blocks * block_rows, HEAD_DIM)
        vals = vals_sc[...]
        half = q_sc.shape[0] // 2
        bias = None
        if masked:
            key_block = first_block + lax.broadcasted_iota(
                jnp.int32, (1, tile_blocks * block_rows), 1
            ) // block_rows
            visible = (key_block >= lo) & (key_block <= hi)
            bias = jnp.where(visible, 0.0, -jnp.inf).astype(jnp.float32)
        for part in range(2):
            rows_here = pl.ds(part * half, half)
            half_step(bias, keys, vals, rows_here)

    def half_step(bias, keys, vals, rows_here):
        scores = lax.dot_general(
            q_sc[rows_here], keys, (((1,), (1,)), ((), ())), preferred_element_type=jnp.float32
        )
        if bias is not None:
            scores = scores + bias
        running_max = m_sc[rows_here]
        new_max = jnp.maximum(running_max, jnp.max(scores, axis=1, keepdims=True))
        raw_weights = jnp.exp2(scores - new_max)
        factor = jnp.exp2(running_max - new_max)
        mixed = jnp.dot(
            raw_weights.astype(jnp.bfloat16), vals, preferred_element_type=jnp.float32
        )
        l_sc[rows_here] = l_sc[rows_here] * factor + mixed[:, HEAD_DIM:HEAD_DIM + 1]
        acc_sc[rows_here] = acc_sc[rows_here] * factor + mixed[:, :HEAD_DIM]
        m_sc[rows_here] = new_max

    active = tile <= hi // tile_blocks
    edge = (first_block < lo) | (first_block + tile_blocks - 1 > hi)

    @pl.when(active & edge)
    def _edge_step():
        step(True)

    @pl.when(active & jnp.logical_not(edge))
    def _inner_step():
        step(False)

    @pl.when(t == last)
    def _done():
        m_out[0] = m_sc[...]
        l_out[0] = l_sc[...]
        acc_out[0] = acc_sc[...]


def attend(bounds, q, kv, half, state=None):
    rows = q.shape[0]
    _, n_blocks, block_rows, _ = kv.shape
    tile_blocks = TILE_KEYS // block_rows
    n_tiles = n_blocks // tile_blocks
    qrows = rows * GROUP

    def tile_of(t, b):
        return jnp.minimum(b[0] // tile_blocks + t, b[1] // tile_blocks)

    in_specs = [
        pl.BlockSpec((rows, GROUP * HEAD_DIM), lambda g, t, b: (0, g)),
        pl.BlockSpec(
            (None, tile_blocks, block_rows, HEAD_DIM),
            lambda g, t, b: (half, tile_of(t, b), 0, g),
        ),
        pl.BlockSpec(
            (None, tile_blocks, block_rows, HEAD_DIM),
            lambda g, t, b: (half, tile_of(t, b), 0, KV_HEADS + g),
        ),
    ]
    operands = [q, kv, kv]
    state_specs = [
        pl.BlockSpec((1, qrows, 1), lambda g, t, b: (g, 0, 0)),
        pl.BlockSpec((1, qrows, 1), lambda g, t, b: (g, 0, 0)),
        pl.BlockSpec((1, qrows, HEAD_DIM), lambda g, t, b: (g, 0, 0)),
    ]
    state_shapes = [
        jax.ShapeDtypeStruct((KV_HEADS, qrows, 1), jnp.float32),
        jax.ShapeDtypeStruct((KV_HEADS, qrows, 1), jnp.float32),
        jax.ShapeDtypeStruct((KV_HEADS, qrows, HEAD_DIM), jnp.float32),
    ]
    if state is not None:
        in_specs += state_specs
        operands += list(state)
    kernel = functools.partial(attend_kernel, carry_in=state is not None)
    tile_flops = 4 * qrows * TILE_KEYS * HEAD_DIM
    cost = pl.CostEstimate(
        flops=KV_HEADS * n_tiles * tile_flops,
        transcendentals=KV_HEADS * n_tiles * qrows * TILE_KEYS,
        bytes_accessed=kv.size + q.size * 2 + KV_HEADS * qrows * HEAD_DIM * 8,
    )
    return pl.pallas_call(
        kernel,
        grid_spec=pltpu.PrefetchScalarGridSpec(
            num_scalar_prefetch=1,
            grid=(KV_HEADS, n_tiles),
            in_specs=in_specs,
            out_specs=state_specs,
            scratch_shapes=[
                pltpu.VMEM((qrows, HEAD_DIM), jnp.bfloat16),
                pltpu.VMEM((qrows, 1), jnp.float32),
                pltpu.VMEM((qrows, 1), jnp.float32),
                pltpu.VMEM((qrows, HEAD_DIM), jnp.float32),
                pltpu.VMEM((TILE_KEYS, 2 * HEAD_DIM), jnp.bfloat16),
            ],
        ),
        out_shape=state_shapes,
        compiler_params=pltpu.CompilerParams(
            dimension_semantics=("arbitrary", "arbitrary"),
        ),
        cost_estimate=cost,
    )(bounds, *operands)


def split_halves(state, own_rows):
    mine, theirs = [], []
    for part in state:
        shaped = part.reshape(KV_HEADS, GROUP, 2, own_rows, part.shape[-1])
        mine.append(shaped[:, :, 0])
        theirs.append(shaped[:, :, 1])
    return mine, theirs


def send_back(theirs, swap):
    run_max, run_sum, acc = theirs
    acc = lax.ppermute(acc.astype(jnp.bfloat16), "row", swap).astype(jnp.float32)
    return [lax.ppermute(run_max, "row", swap), lax.ppermute(run_sum, "row", swap), acc]


def finish(mine, theirs, gain):
    own_max, own_sum, own_acc = mine
    far_max, far_sum, far_acc = theirs
    top = jnp.maximum(own_max, far_max)
    own_factor = jnp.exp2(own_max - top)
    far_factor = jnp.exp2(far_max - top)
    total = own_sum * own_factor + far_sum * far_factor
    acc = own_acc * own_factor + far_acc * far_factor
    mixed = acc / total
    spread = jnp.sqrt(jnp.mean(mixed * mixed, axis=-1, keepdims=True) + 1e-06)
    normed = (mixed / spread * gain).astype(jnp.bfloat16)
    rows = normed.shape[2]
    return normed.transpose(2, 0, 1, 3).reshape(rows, KV_HEADS * GROUP * HEAD_DIM)


def per_device(queries, keys, values, gain, outer, inner):
    seq_index = lax.axis_index("outer") * inner + lax.axis_index("inner")
    last_index = outer * inner - 1
    own_rows = queries.shape[2]
    swap = [(0, 1), (1, 0)]
    partner_queries = lax.ppermute(queries, "row", swap)
    both_queries = jnp.concatenate([queries, partner_queries], axis=2)
    pair = jnp.concatenate([keys, values], axis=-1)
    blocks = lax.all_gather(pair[:, 0], "outer", axis=1, tiled=False)
    blocks = lax.all_gather(blocks, "inner", axis=2, tiled=False)
    blocks = blocks.reshape(2, outer * inner, own_rows, pair.shape[3])
    zero = jnp.int32(0)
    top = jnp.int32(last_index)

    early = attend(jnp.stack([zero, seq_index]), both_queries[0, 0], blocks, 0)
    early_mine, early_theirs = split_halves(early, own_rows)
    early_back = send_back(early_theirs, swap)

    state = attend(jnp.stack([zero, top]), both_queries[1, 0], blocks, 0)
    late = attend(jnp.stack([seq_index, top]), both_queries[1, 0], blocks, 1, state=state)
    late_mine, late_theirs = split_halves(late, own_rows)
    late_back = send_back(late_theirs, swap)

    early_out = finish(early_mine, early_back, gain)
    late_out = finish(late_mine, late_back, gain)
    return jnp.stack([early_out, late_out]).reshape(2, 1, own_rows, KV_HEADS * GROUP * HEAD_DIM)


def solution(mesh):
    seq_count, row_count = mesh.devices.shape
    outer = math.gcd(seq_count, 4)
    inner = seq_count // outer
    split = Mesh(mesh.devices.reshape(outer, inner, row_count), ("outer", "inner", "row"))
    spec = P(None, ("outer", "inner"), "row", None)
    return jax.shard_map(
        functools.partial(per_device, outer=outer, inner=inner),
        mesh=split,
        in_specs=(spec, spec, spec, P()),
        out_specs=spec,
        check_vma=False,
    )
```

```python
import functools
import math

import jax
import jax.numpy as jnp
from jax import lax
from jax.experimental import pallas as pl
from jax.experimental.pallas import tpu as pltpu
from jax.sharding import Mesh, PartitionSpec as P

KV_HEADS = 4
GROUP = 6
HEAD_DIM = 128
TILE_KEYS = 1024

lowest_score = -1e30
EXP2_SCALE = math.log2(math.e) / math.sqrt(HEAD_DIM)


def attend_kernel(bounds_ref, q_ref, k_ref, v_ref, *rest, carry_in):
    if carry_in:
        stats_in, acc_in = rest[:2]
        rest = rest[2:]
    stats_out, acc_out = rest[:2]
    q_sc, m_sc, l_sc, acc_sc, vals_sc = rest[2:]

    t = pl.program_id(1)
    last = pl.num_programs(1) - 1
    tile_blocks, block_rows, _ = k_ref.shape
    lo = bounds_ref[0]
    hi = bounds_ref[1]
    tile = lo // tile_blocks + t
    first_block = tile * tile_blocks

    @pl.when(t == 0)
    def _init():
        vals_sc[:, HEAD_DIM:] = jnp.ones((vals_sc.shape[0], HEAD_DIM), jnp.bfloat16)
        q_sc[...] = jnp.concatenate(
            [q_ref[:, j * HEAD_DIM:(j + 1) * HEAD_DIM] for j in range(GROUP)], axis=0
        )
        if carry_in:
            m_sc[...] = stats_in[0][:, 0:1]
            l_sc[...] = stats_in[0][:, 1:2]
            acc_sc[...] = acc_in[0]
        else:
            m_sc[...] = jnp.full(m_sc.shape, lowest_score, jnp.float32)
            l_sc[...] = jnp.zeros(l_sc.shape, jnp.float32)
            acc_sc[...] = jnp.zeros(acc_sc.shape, jnp.float32)

    def step(masked):
        keys = k_ref[...].reshape(tile_blocks * block_rows, HEAD_DIM)
        vals_sc[:, :HEAD_DIM] = v_ref[...].reshape(tile_blocks * block_rows, HEAD_DIM)
        vals = vals_sc[...]
        half = q_sc.shape[0] // 2
        bias = None
        if masked:
            key_block = first_block + lax.broadcasted_iota(
                jnp.int32, (1, tile_blocks * block_rows), 1
            ) // block_rows
            visible = (key_block >= lo) & (key_block <= hi)
            bias = jnp.where(visible, 0.0, -jnp.inf).astype(jnp.float32)
        for part in range(2):
            rows_here = pl.ds(part * half, half)
            half_step(bias, keys, vals, rows_here)

    def half_step(bias, keys, vals, rows_here):
        scores = lax.dot_general(
            q_sc[rows_here], keys, (((1,), (1,)), ((), ())), preferred_element_type=jnp.float32
        )
        if bias is not None:
            scores = scores + bias
        running_max = m_sc[rows_here]
        new_max = jnp.maximum(running_max, jnp.max(scores, axis=1, keepdims=True))
        raw_weights = jnp.exp2((scores - new_max) * EXP2_SCALE)
        factor = jnp.exp2((running_max - new_max) * EXP2_SCALE)
        mixed = jnp.dot(
            raw_weights.astype(jnp.bfloat16), vals, preferred_element_type=jnp.float32
        )
        l_sc[rows_here] = l_sc[rows_here] * factor + mixed[:, HEAD_DIM:HEAD_DIM + 1]
        acc_sc[rows_here] = acc_sc[rows_here] * factor + mixed[:, :HEAD_DIM]
        m_sc[rows_here] = new_max

    active = tile <= hi // tile_blocks
    edge = (first_block < lo) | (first_block + tile_blocks - 1 > hi)

    @pl.when(active & edge)
    def _edge_step():
        step(True)

    @pl.when(active & jnp.logical_not(edge))
    def _inner_step():
        step(False)

    @pl.when(t == last)
    def _done():
        column = lax.broadcasted_iota(jnp.int32, (m_sc.shape[0], HEAD_DIM), 1)
        stats_out[0] = jnp.where(column == 0, m_sc[...], jnp.where(column == 1, l_sc[...], 0.0))
        acc_out[0] = acc_sc[...]


def attend(bounds, q, kv, half, state=None):
    rows = q.shape[0]
    _, n_blocks, block_rows, _ = kv.shape
    tile_blocks = TILE_KEYS // block_rows
    n_tiles = n_blocks // tile_blocks
    qrows = rows * GROUP

    def tile_of(t, b):
        return jnp.minimum(b[0] // tile_blocks + t, b[1] // tile_blocks)

    in_specs = [
        pl.BlockSpec((rows, GROUP * HEAD_DIM), lambda g, t, b: (0, g)),
        pl.BlockSpec(
            (None, tile_blocks, block_rows, HEAD_DIM),
            lambda g, t, b: (half, tile_of(t, b), 0, g),
        ),
        pl.BlockSpec(
            (None, tile_blocks, block_rows, HEAD_DIM),
            lambda g, t, b: (half, tile_of(t, b), 0, KV_HEADS + g),
        ),
    ]
    operands = [q, kv, kv]
    state_specs = [
        pl.BlockSpec((1, qrows, HEAD_DIM), lambda g, t, b: (g, 0, 0)),
        pl.BlockSpec((1, qrows, HEAD_DIM), lambda g, t, b: (g, 0, 0)),
    ]
    state_shapes = [
        jax.ShapeDtypeStruct((KV_HEADS, qrows, HEAD_DIM), jnp.float32),
        jax.ShapeDtypeStruct((KV_HEADS, qrows, HEAD_DIM), jnp.float32),
    ]
    if state is not None:
        in_specs += state_specs
        operands += list(state)
    kernel = functools.partial(attend_kernel, carry_in=state is not None)
    tile_flops = 4 * qrows * TILE_KEYS * HEAD_DIM
    cost = pl.CostEstimate(
        flops=KV_HEADS * n_tiles * tile_flops,
        transcendentals=KV_HEADS * n_tiles * qrows * TILE_KEYS,
        bytes_accessed=kv.size + q.size * 2 + KV_HEADS * qrows * HEAD_DIM * 8,
    )
    return pl.pallas_call(
        kernel,
        grid_spec=pltpu.PrefetchScalarGridSpec(
            num_scalar_prefetch=1,
            grid=(KV_HEADS, n_tiles),
            in_specs=in_specs,
            out_specs=state_specs,
            scratch_shapes=[
                pltpu.VMEM((qrows, HEAD_DIM), jnp.bfloat16),
                pltpu.VMEM((qrows, 1), jnp.float32),
                pltpu.VMEM((qrows, 1), jnp.float32),
                pltpu.VMEM((qrows, HEAD_DIM), jnp.float32),
                pltpu.VMEM((TILE_KEYS, 2 * HEAD_DIM), jnp.bfloat16),
            ],
        ),
        out_shape=state_shapes,
        compiler_params=pltpu.CompilerParams(
            dimension_semantics=("arbitrary", "arbitrary"),
        ),
        cost_estimate=cost,
    )(bounds, *operands)


def split_halves(state, own_rows):
    stats, acc = (part.reshape(KV_HEADS, GROUP, 2, own_rows, HEAD_DIM) for part in state)
    mine = [stats[:, :, 0, :, 0:1], stats[:, :, 0, :, 1:2], acc[:, :, 0]]
    theirs = [stats[:, :, 1, :, 0:2], acc[:, :, 1]]
    return mine, theirs


def send_back(theirs, swap):
    stats, acc = theirs
    acc = lax.ppermute(acc.astype(jnp.bfloat16), "row", swap).astype(jnp.float32)
    stats = lax.ppermute(stats, "row", swap)
    return [stats[..., 0:1], stats[..., 1:2], acc]


def finish(mine, theirs, gain):
    own_max, own_sum, own_acc = mine
    far_max, far_sum, far_acc = theirs
    top = jnp.maximum(own_max, far_max)
    own_factor = jnp.exp2((own_max - top) * EXP2_SCALE)
    far_factor = jnp.exp2((far_max - top) * EXP2_SCALE)
    total = own_sum * own_factor + far_sum * far_factor
    acc = own_acc * own_factor + far_acc * far_factor
    mixed = acc / total
    spread = jnp.sqrt(jnp.mean(mixed * mixed, axis=-1, keepdims=True) + 1e-06)
    normed = (mixed / spread * gain).astype(jnp.bfloat16)
    rows = normed.shape[2]
    return normed.transpose(2, 0, 1, 3).reshape(rows, KV_HEADS * GROUP * HEAD_DIM)


def per_device(queries, keys, values, gain, outer, inner):
    seq_index = lax.axis_index("outer") * inner + lax.axis_index("inner")
    last_index = outer * inner - 1
    own_rows = queries.shape[2]
    swap = [(0, 1), (1, 0)]
    partner_queries = lax.ppermute(queries, "row", swap)
    both_queries = jnp.concatenate([queries, partner_queries], axis=2)
    pair = jnp.concatenate([keys, values], axis=-1)
    blocks = lax.all_gather(pair[:, 0], "outer", axis=1, tiled=False)
    blocks = lax.all_gather(blocks, "inner", axis=2, tiled=False)
    blocks = blocks.reshape(2, outer * inner, own_rows, pair.shape[3])
    zero = jnp.int32(0)
    top = jnp.int32(last_index)

    early = attend(jnp.stack([zero, seq_index]), both_queries[0, 0], blocks, 0)
    early_mine, early_theirs = split_halves(early, own_rows)
    early_back = send_back(early_theirs, swap)

    state = attend(jnp.stack([zero, top]), both_queries[1, 0], blocks, 0)
    late = attend(jnp.stack([seq_index, top]), both_queries[1, 0], blocks, 1, state=state)
    late_mine, late_theirs = split_halves(late, own_rows)
    late_back = send_back(late_theirs, swap)

    early_out = finish(early_mine, early_back, gain)
    late_out = finish(late_mine, late_back, gain)
    return jnp.stack([early_out, late_out]).reshape(2, 1, own_rows, KV_HEADS * GROUP * HEAD_DIM)


def solution(mesh):
    seq_count, row_count = mesh.devices.shape
    outer = math.gcd(seq_count, 4)
    inner = seq_count // outer
    split = Mesh(mesh.devices.reshape(outer, inner, row_count), ("outer", "inner", "row"))
    spec = P(None, ("outer", "inner"), "row", None)
    return jax.shard_map(
        functools.partial(per_device, outer=outer, inner=inner),
        mesh=split,
        in_specs=(spec, spec, spec, P()),
        out_specs=spec,
        check_vma=False,
    )
```

```python
import functools
import math

import jax
import jax.numpy as jnp
from jax import lax
from jax.experimental import pallas as pl
from jax.experimental.pallas import tpu as pltpu
from jax.sharding import Mesh, PartitionSpec as P

KV_HEADS = 4
GROUP = 6
HEAD_DIM = 128
TILE_KEYS = 1024

lowest_score = -1e30
EXP2_SCALE = math.log2(math.e) / math.sqrt(HEAD_DIM)


def attend_kernel(bounds_ref, q_ref, k_ref, v_ref, *rest, carry_in):
    if carry_in:
        m_in, l_in, acc_in = rest[:3]
        rest = rest[3:]
    m_out, l_out, acc_out = rest[:3]
    q_sc, m_sc, l_sc, acc_sc, vals_sc = rest[3:]

    t = pl.program_id(1)
    last = pl.num_programs(1) - 1
    tile_blocks, block_rows, _ = k_ref.shape
    lo = bounds_ref[0]
    hi = bounds_ref[1]
    tile = lo // tile_blocks + t
    first_block = tile * tile_blocks

    @pl.when(t == 0)
    def _init():
        vals_sc[:, HEAD_DIM:] = jnp.ones((vals_sc.shape[0], HEAD_DIM), jnp.bfloat16)
        q_sc[...] = jnp.concatenate(
            [q_ref[:, j * HEAD_DIM:(j + 1) * HEAD_DIM] for j in range(GROUP)], axis=0
        )
        if carry_in:
            m_sc[...] = m_in[0]
            l_sc[...] = l_in[0]
            acc_sc[...] = acc_in[0]
        else:
            m_sc[...] = jnp.full(m_sc.shape, lowest_score, jnp.float32)
            l_sc[...] = jnp.zeros(l_sc.shape, jnp.float32)
            acc_sc[...] = jnp.zeros(acc_sc.shape, jnp.float32)

    def step(masked):
        keys = k_ref[...].reshape(tile_blocks * block_rows, HEAD_DIM)
        vals_sc[:, :HEAD_DIM] = v_ref[...].reshape(tile_blocks * block_rows, HEAD_DIM)
        vals = vals_sc[...]
        half = q_sc.shape[0] // 2
        bias = None
        if masked:
            key_block = first_block + lax.broadcasted_iota(
                jnp.int32, (1, tile_blocks * block_rows), 1
            ) // block_rows
            visible = (key_block >= lo) & (key_block <= hi)
            bias = jnp.where(visible, 0.0, -jnp.inf).astype(jnp.float32)
        for part in range(2):
            rows_here = pl.ds(part * half, half)
            half_step(bias, keys, vals, rows_here)

    def half_step(bias, keys, vals, rows_here):
        scores = lax.dot_general(
            q_sc[rows_here], keys, (((1,), (1,)), ((), ())), preferred_element_type=jnp.float32
        )
        if bias is not None:
            scores = scores + bias
        running_max = m_sc[rows_here]
        new_max = jnp.maximum(running_max, jnp.max(scores, axis=1, keepdims=True))
        raw_weights = jnp.exp2((scores - new_max) * EXP2_SCALE)
        factor = jnp.exp2((running_max - new_max) * EXP2_SCALE)
        mixed = jnp.dot(
            raw_weights.astype(jnp.bfloat16), vals, preferred_element_type=jnp.float32
        )
        l_sc[rows_here] = l_sc[rows_here] * factor + mixed[:, HEAD_DIM:HEAD_DIM + 1]
        acc_sc[rows_here] = acc_sc[rows_here] * factor + mixed[:, :HEAD_DIM]
        m_sc[rows_here] = new_max

    active = tile <= hi // tile_blocks
    edge = (first_block < lo) | (first_block + tile_blocks - 1 > hi)

    @pl.when(active & edge)
    def _edge_step():
        step(True)

    @pl.when(active & jnp.logical_not(edge))
    def _inner_step():
        step(False)

    @pl.when(t == last)
    def _done():
        m_out[0] = m_sc[...]
        l_out[0] = l_sc[...]
        acc_out[0] = acc_sc[...]


def attend(bounds, q, kv, half, state=None):
    rows = q.shape[0]
    _, n_blocks, block_rows, _ = kv.shape
    tile_blocks = TILE_KEYS // block_rows
    n_tiles = n_blocks // tile_blocks
    qrows = rows * GROUP

    def tile_of(t, b):
        return jnp.minimum(b[0] // tile_blocks + t, b[1] // tile_blocks)

    in_specs = [
        pl.BlockSpec((rows, GROUP * HEAD_DIM), lambda g, t, b: (0, g)),
        pl.BlockSpec(
            (None, tile_blocks, block_rows, HEAD_DIM),
            lambda g, t, b: (half, tile_of(t, b), 0, g),
        ),
        pl.BlockSpec(
            (None, tile_blocks, block_rows, HEAD_DIM),
            lambda g, t, b: (half, tile_of(t, b), 0, KV_HEADS + g),
        ),
    ]
    operands = [q, kv, kv]
    state_specs = [
        pl.BlockSpec((1, qrows, 1), lambda g, t, b: (g, 0, 0)),
        pl.BlockSpec((1, qrows, 1), lambda g, t, b: (g, 0, 0)),
        pl.BlockSpec((1, qrows, HEAD_DIM), lambda g, t, b: (g, 0, 0)),
    ]
    state_shapes = [
        jax.ShapeDtypeStruct((KV_HEADS, qrows, 1), jnp.float32),
        jax.ShapeDtypeStruct((KV_HEADS, qrows, 1), jnp.float32),
        jax.ShapeDtypeStruct((KV_HEADS, qrows, HEAD_DIM), jnp.float32),
    ]
    if state is not None:
        in_specs += state_specs
        operands += list(state)
    kernel = functools.partial(attend_kernel, carry_in=state is not None)
    tile_flops = 4 * qrows * TILE_KEYS * HEAD_DIM
    cost = pl.CostEstimate(
        flops=KV_HEADS * n_tiles * tile_flops,
        transcendentals=KV_HEADS * n_tiles * qrows * TILE_KEYS,
        bytes_accessed=kv.size + q.size * 2 + KV_HEADS * qrows * HEAD_DIM * 8,
    )
    return pl.pallas_call(
        kernel,
        grid_spec=pltpu.PrefetchScalarGridSpec(
            num_scalar_prefetch=1,
            grid=(KV_HEADS, n_tiles),
            in_specs=in_specs,
            out_specs=state_specs,
            scratch_shapes=[
                pltpu.VMEM((qrows, HEAD_DIM), jnp.bfloat16),
                pltpu.VMEM((qrows, 1), jnp.float32),
                pltpu.VMEM((qrows, 1), jnp.float32),
                pltpu.VMEM((qrows, HEAD_DIM), jnp.float32),
                pltpu.VMEM((TILE_KEYS, 2 * HEAD_DIM), jnp.bfloat16),
            ],
        ),
        out_shape=state_shapes,
        compiler_params=pltpu.CompilerParams(
            dimension_semantics=("arbitrary", "arbitrary"),
        ),
        cost_estimate=cost,
    )(bounds, *operands)


def split_halves(state, own_rows):
    mine, theirs = [], []
    for part in state:
        shaped = part.reshape(KV_HEADS, GROUP, 2, own_rows, part.shape[-1])
        mine.append(shaped[:, :, 0])
        theirs.append(shaped[:, :, 1])
    return mine, theirs


def send_back(theirs, swap):
    run_max, run_sum, acc = theirs
    acc = lax.ppermute(acc.astype(jnp.bfloat16), "row", swap).astype(jnp.float32)
    stats = lax.ppermute(jnp.concatenate([run_max, run_sum], axis=-1), "row", swap)
    return [stats[..., 0:1], stats[..., 1:2], acc]


def finish(mine, theirs, gain):
    own_max, own_sum, own_acc = mine
    far_max, far_sum, far_acc = theirs
    top = jnp.maximum(own_max, far_max)
    own_factor = jnp.exp2((own_max - top) * EXP2_SCALE)
    far_factor = jnp.exp2((far_max - top) * EXP2_SCALE)
    total = own_sum * own_factor + far_sum * far_factor
    acc = own_acc * own_factor + far_acc * far_factor
    mixed = acc / total
    spread = jnp.sqrt(jnp.mean(mixed * mixed, axis=-1, keepdims=True) + 1e-06)
    normed = (mixed / spread * gain).astype(jnp.bfloat16)
    rows = normed.shape[2]
    return normed.transpose(2, 0, 1, 3).reshape(rows, KV_HEADS * GROUP * HEAD_DIM)


def per_device(queries, keys, values, gain, outer, inner):
    seq_index = lax.axis_index("outer") * inner + lax.axis_index("inner")
    last_index = outer * inner - 1
    own_rows = queries.shape[2]
    swap = [(0, 1), (1, 0)]
    partner_queries = lax.ppermute(queries, "row", swap)
    both_queries = jnp.concatenate([queries, partner_queries], axis=2)
    pair = jnp.concatenate([keys, values], axis=-1)
    blocks = lax.all_gather(pair[:, 0], "outer", axis=1, tiled=False)
    blocks = lax.all_gather(blocks, "inner", axis=2, tiled=False)
    blocks = blocks.reshape(2, outer * inner, own_rows, pair.shape[3])
    zero = jnp.int32(0)
    top = jnp.int32(last_index)

    early = attend(jnp.stack([zero, seq_index]), both_queries[0, 0], blocks, 0)
    early_mine, early_theirs = split_halves(early, own_rows)
    early_back = send_back(early_theirs, swap)

    state = attend(jnp.stack([zero, top]), both_queries[1, 0], blocks, 0)
    late = attend(jnp.stack([seq_index, top]), both_queries[1, 0], blocks, 1, state=state)
    late_mine, late_theirs = split_halves(late, own_rows)
    late_back = send_back(late_theirs, swap)

    early_out = finish(early_mine, early_back, gain)
    late_out = finish(late_mine, late_back, gain)
    return jnp.stack([early_out, late_out]).reshape(2, 1, own_rows, KV_HEADS * GROUP * HEAD_DIM)


def solution(mesh):
    seq_count, row_count = mesh.devices.shape
    outer = math.gcd(seq_count, 4)
    inner = seq_count // outer
    split = Mesh(mesh.devices.reshape(outer, inner, row_count), ("outer", "inner", "row"))
    spec = P(None, ("outer", "inner"), "row", None)
    return jax.shard_map(
        functools.partial(per_device, outer=outer, inner=inner),
        mesh=split,
        in_specs=(spec, spec, spec, P()),
        out_specs=spec,
        check_vma=False,
    )
```

```python
import functools
import math

import jax
import jax.numpy as jnp
from jax import lax
from jax.experimental import pallas as pl
from jax.experimental.pallas import tpu as pltpu
from jax.sharding import Mesh, PartitionSpec as P

KV_HEADS = 4
GROUP = 6
HEAD_DIM = 128
TILE_KEYS = 1024

lowest_score = -1e30
EXP2_SCALE = math.log2(math.e) / math.sqrt(HEAD_DIM)


def attend_kernel(bounds_ref, q_ref, k_ref, v_ref, *rest, carry_in, tiles_per_phase):
    if carry_in:
        m_in, l_in, acc_in = rest[:3]
        rest = rest[3:]
    m_out, l_out, acc_out = rest[:3]
    q_sc, m_sc, l_sc, acc_sc, vals_sc = rest[3:]

    t = pl.program_id(1)
    last = pl.num_programs(1) - 1
    tile_blocks, block_rows, _ = k_ref.shape
    phase = t // tiles_per_phase
    lo = bounds_ref[2 * phase]
    hi = bounds_ref[2 * phase + 1]
    tile = lo // tile_blocks + t % tiles_per_phase
    first_block = tile * tile_blocks

    @pl.when(t == 0)
    def _init():
        vals_sc[:, HEAD_DIM:] = jnp.ones((vals_sc.shape[0], HEAD_DIM), jnp.bfloat16)
        q_sc[...] = jnp.concatenate(
            [q_ref[:, j * HEAD_DIM:(j + 1) * HEAD_DIM] for j in range(GROUP)], axis=0
        )
        if carry_in:
            m_sc[...] = m_in[0]
            l_sc[...] = l_in[0]
            acc_sc[...] = acc_in[0]
        else:
            m_sc[...] = jnp.full(m_sc.shape, lowest_score, jnp.float32)
            l_sc[...] = jnp.zeros(l_sc.shape, jnp.float32)
            acc_sc[...] = jnp.zeros(acc_sc.shape, jnp.float32)

    def step(masked):
        keys = k_ref[...].reshape(tile_blocks * block_rows, HEAD_DIM)
        vals_sc[:, :HEAD_DIM] = v_ref[...].reshape(tile_blocks * block_rows, HEAD_DIM)
        vals = vals_sc[...]
        half = q_sc.shape[0] // 2
        bias = None
        if masked:
            key_block = first_block + lax.broadcasted_iota(
                jnp.int32, (1, tile_blocks * block_rows), 1
            ) // block_rows
            visible = (key_block >= lo) & (key_block <= hi)
            bias = jnp.where(visible, 0.0, -jnp.inf).astype(jnp.float32)
        for part in range(2):
            rows_here = pl.ds(part * half, half)
            half_step(bias, keys, vals, rows_here)

    def half_step(bias, keys, vals, rows_here):
        scores = lax.dot_general(
            q_sc[rows_here], keys, (((1,), (1,)), ((), ())), preferred_element_type=jnp.float32
        )
        if bias is not None:
            scores = scores + bias
        running_max = m_sc[rows_here]
        new_max = jnp.maximum(running_max, jnp.max(scores, axis=1, keepdims=True))
        raw_weights = jnp.exp2((scores - new_max) * EXP2_SCALE)
        factor = jnp.exp2((running_max - new_max) * EXP2_SCALE)
        mixed = jnp.dot(
            raw_weights.astype(jnp.bfloat16), vals, preferred_element_type=jnp.float32
        )
        l_sc[rows_here] = l_sc[rows_here] * factor + mixed[:, HEAD_DIM:HEAD_DIM + 1]
        acc_sc[rows_here] = acc_sc[rows_here] * factor + mixed[:, :HEAD_DIM]
        m_sc[rows_here] = new_max

    active = tile <= hi // tile_blocks
    edge = (first_block < lo) | (first_block + tile_blocks - 1 > hi)

    @pl.when(active & edge)
    def _edge_step():
        step(True)

    @pl.when(active & jnp.logical_not(edge))
    def _inner_step():
        step(False)

    @pl.when(t == last)
    def _done():
        m_out[0] = m_sc[...]
        l_out[0] = l_sc[...]
        acc_out[0] = acc_sc[...]


def attend(bounds, q, kv, halves, state=None):
    rows = q.shape[0]
    _, n_blocks, block_rows, _ = kv.shape
    tile_blocks = TILE_KEYS // block_rows
    n_tiles = n_blocks // tile_blocks
    qrows = rows * GROUP

    phases = len(halves)

    def half_of(t):
        return halves[0] if phases == 1 else t // n_tiles

    def tile_of(t, b):
        phase = t // n_tiles
        first = b[2 * phase] // tile_blocks + t % n_tiles
        return jnp.minimum(first, b[2 * phase + 1] // tile_blocks)

    in_specs = [
        pl.BlockSpec((rows, GROUP * HEAD_DIM), lambda g, t, b: (0, g)),
        pl.BlockSpec(
            (None, tile_blocks, block_rows, HEAD_DIM),
            lambda g, t, b: (half_of(t), tile_of(t, b), 0, g),
        ),
        pl.BlockSpec(
            (None, tile_blocks, block_rows, HEAD_DIM),
            lambda g, t, b: (half_of(t), tile_of(t, b), 0, KV_HEADS + g),
        ),
    ]
    operands = [q, kv, kv]
    state_specs = [
        pl.BlockSpec((1, qrows, 1), lambda g, t, b: (g, 0, 0)),
        pl.BlockSpec((1, qrows, 1), lambda g, t, b: (g, 0, 0)),
        pl.BlockSpec((1, qrows, HEAD_DIM), lambda g, t, b: (g, 0, 0)),
    ]
    state_shapes = [
        jax.ShapeDtypeStruct((KV_HEADS, qrows, 1), jnp.float32),
        jax.ShapeDtypeStruct((KV_HEADS, qrows, 1), jnp.float32),
        jax.ShapeDtypeStruct((KV_HEADS, qrows, HEAD_DIM), jnp.float32),
    ]
    if state is not None:
        in_specs += state_specs
        operands += list(state)
    kernel = functools.partial(
        attend_kernel, carry_in=state is not None, tiles_per_phase=n_tiles
    )
    tile_flops = 4 * qrows * TILE_KEYS * HEAD_DIM
    cost = pl.CostEstimate(
        flops=KV_HEADS * n_tiles * phases * tile_flops,
        transcendentals=KV_HEADS * n_tiles * phases * qrows * TILE_KEYS,
        bytes_accessed=kv.size + q.size * 2 + KV_HEADS * qrows * HEAD_DIM * 8,
    )
    return pl.pallas_call(
        kernel,
        grid_spec=pltpu.PrefetchScalarGridSpec(
            num_scalar_prefetch=1,
            grid=(KV_HEADS, n_tiles * phases),
            in_specs=in_specs,
            out_specs=state_specs,
            scratch_shapes=[
                pltpu.VMEM((qrows, HEAD_DIM), jnp.bfloat16),
                pltpu.VMEM((qrows, 1), jnp.float32),
                pltpu.VMEM((qrows, 1), jnp.float32),
                pltpu.VMEM((qrows, HEAD_DIM), jnp.float32),
                pltpu.VMEM((TILE_KEYS, 2 * HEAD_DIM), jnp.bfloat16),
            ],
        ),
        out_shape=state_shapes,
        compiler_params=pltpu.CompilerParams(
            dimension_semantics=("arbitrary", "arbitrary"),
        ),
        cost_estimate=cost,
    )(bounds, *operands)


def split_halves(state, own_rows):
    mine, theirs = [], []
    for part in state:
        shaped = part.reshape(KV_HEADS, GROUP, 2, own_rows, part.shape[-1])
        mine.append(shaped[:, :, 0])
        theirs.append(shaped[:, :, 1])
    return mine, theirs


def send_back(theirs, swap):
    run_max, run_sum, acc = theirs
    acc = lax.ppermute(acc.astype(jnp.bfloat16), "row", swap).astype(jnp.float32)
    stats = lax.ppermute(jnp.concatenate([run_max, run_sum], axis=-1), "row", swap)
    return [stats[..., 0:1], stats[..., 1:2], acc]


def finish(mine, theirs, gain):
    own_max, own_sum, own_acc = mine
    far_max, far_sum, far_acc = theirs
    top = jnp.maximum(own_max, far_max)
    own_factor = jnp.exp2((own_max - top) * EXP2_SCALE)
    far_factor = jnp.exp2((far_max - top) * EXP2_SCALE)
    total = own_sum * own_factor + far_sum * far_factor
    acc = own_acc * own_factor + far_acc * far_factor
    mixed = acc / total
    spread = jnp.sqrt(jnp.mean(mixed * mixed, axis=-1, keepdims=True) + 1e-06)
    normed = (mixed / spread * gain).astype(jnp.bfloat16)
    rows = normed.shape[2]
    return normed.transpose(2, 0, 1, 3).reshape(rows, KV_HEADS * GROUP * HEAD_DIM)


def per_device(queries, keys, values, gain, outer, inner):
    seq_index = lax.axis_index("outer") * inner + lax.axis_index("inner")
    last_index = outer * inner - 1
    own_rows = queries.shape[2]
    swap = [(0, 1), (1, 0)]
    partner_queries = lax.ppermute(queries, "row", swap)
    both_queries = jnp.concatenate([queries, partner_queries], axis=2)
    pair = jnp.concatenate([keys, values], axis=-1)
    blocks = lax.all_gather(pair[:, 0], "outer", axis=1, tiled=False)
    blocks = lax.all_gather(blocks, "inner", axis=2, tiled=False)
    blocks = blocks.reshape(2, outer * inner, own_rows, pair.shape[3])
    zero = jnp.int32(0)
    top = jnp.int32(last_index)

    early = attend(jnp.stack([zero, seq_index]), both_queries[0, 0], blocks, (0,))
    early_mine, early_theirs = split_halves(early, own_rows)
    early_back = send_back(early_theirs, swap)

    late = attend(
        jnp.stack([zero, top, seq_index, top]), both_queries[1, 0], blocks, (0, 1)
    )
    late_mine, late_theirs = split_halves(late, own_rows)
    late_back = send_back(late_theirs, swap)

    early_out = finish(early_mine, early_back, gain)
    late_out = finish(late_mine, late_back, gain)
    return jnp.stack([early_out, late_out]).reshape(2, 1, own_rows, KV_HEADS * GROUP * HEAD_DIM)


def solution(mesh):
    seq_count, row_count = mesh.devices.shape
    outer = math.gcd(seq_count, 4)
    inner = seq_count // outer
    split = Mesh(mesh.devices.reshape(outer, inner, row_count), ("outer", "inner", "row"))
    spec = P(None, ("outer", "inner"), "row", None)
    return jax.shard_map(
        functools.partial(per_device, outer=outer, inner=inner),
        mesh=split,
        in_specs=(spec, spec, spec, P()),
        out_specs=spec,
        check_vma=False,
    )
```

```python
import functools
import math

import jax
import jax.numpy as jnp
from jax import lax
from jax.experimental import pallas as pl
from jax.experimental.pallas import tpu as pltpu
from jax.sharding import Mesh, PartitionSpec as P

KV_HEADS = 4
GROUP = 6
HEAD_DIM = 128
TILE_KEYS = 1024

lowest_score = -1e30
EXP2_SCALE = math.log2(math.e) / math.sqrt(HEAD_DIM)


def to_row(column):
    return jnp.transpose(jnp.broadcast_to(column, (column.shape[0], HEAD_DIM)))[0:1, :]


def from_row(row):
    return jnp.transpose(jnp.broadcast_to(row, (HEAD_DIM, row.shape[1])))[:, 0:1]


def attend_kernel(bounds_ref, q_ref, k_ref, v_ref, *rest, carry_in, tiles_per_phase):
    if carry_in:
        m_in, l_in, acc_in = rest[:3]
        rest = rest[3:]
    m_out, l_out, acc_out = rest[:3]
    q_sc, m_sc, l_sc, acc_sc, vals_sc = rest[3:]

    t = pl.program_id(1)
    last = pl.num_programs(1) - 1
    tile_blocks, block_rows, _ = k_ref.shape
    phase = t // tiles_per_phase
    lo = bounds_ref[2 * phase]
    hi = bounds_ref[2 * phase + 1]
    tile = lo // tile_blocks + t % tiles_per_phase
    first_block = tile * tile_blocks

    @pl.when(t == 0)
    def _init():
        vals_sc[:, HEAD_DIM:] = jnp.ones((vals_sc.shape[0], HEAD_DIM), jnp.bfloat16)
        q_sc[...] = jnp.concatenate(
            [q_ref[:, j * HEAD_DIM:(j + 1) * HEAD_DIM] for j in range(GROUP)], axis=0
        )
        if carry_in:
            m_sc[...] = from_row(m_in[0])
            l_sc[...] = from_row(l_in[0])
            acc_sc[...] = acc_in[0]
        else:
            m_sc[...] = jnp.full(m_sc.shape, lowest_score, jnp.float32)
            l_sc[...] = jnp.zeros(l_sc.shape, jnp.float32)
            acc_sc[...] = jnp.zeros(acc_sc.shape, jnp.float32)

    def step(masked):
        keys = k_ref[...].reshape(tile_blocks * block_rows, HEAD_DIM)
        vals_sc[:, :HEAD_DIM] = v_ref[...].reshape(tile_blocks * block_rows, HEAD_DIM)
        vals = vals_sc[...]
        half = q_sc.shape[0] // 2
        bias = None
        if masked:
            key_block = first_block + lax.broadcasted_iota(
                jnp.int32, (1, tile_blocks * block_rows), 1
            ) // block_rows
            visible = (key_block >= lo) & (key_block <= hi)
            bias = jnp.where(visible, 0.0, -jnp.inf).astype(jnp.float32)
        for part in range(2):
            rows_here = pl.ds(part * half, half)
            half_step(bias, keys, vals, rows_here)

    def half_step(bias, keys, vals, rows_here):
        scores = lax.dot_general(
            q_sc[rows_here], keys, (((1,), (1,)), ((), ())), preferred_element_type=jnp.float32
        )
        if bias is not None:
            scores = scores + bias
        running_max = m_sc[rows_here]
        new_max = jnp.maximum(running_max, jnp.max(scores, axis=1, keepdims=True))
        raw_weights = jnp.exp2((scores - new_max) * EXP2_SCALE)
        factor = jnp.exp2((running_max - new_max) * EXP2_SCALE)
        mixed = jnp.dot(
            raw_weights.astype(jnp.bfloat16), vals, preferred_element_type=jnp.float32
        )
        l_sc[rows_here] = l_sc[rows_here] * factor + mixed[:, HEAD_DIM:HEAD_DIM + 1]
        acc_sc[rows_here] = acc_sc[rows_here] * factor + mixed[:, :HEAD_DIM]
        m_sc[rows_here] = new_max

    active = tile <= hi // tile_blocks
    edge = (first_block < lo) | (first_block + tile_blocks - 1 > hi)

    @pl.when(active & edge)
    def _edge_step():
        step(True)

    @pl.when(active & jnp.logical_not(edge))
    def _inner_step():
        step(False)

    @pl.when(t == last)
    def _done():
        m_out[0] = to_row(m_sc[...])
        l_out[0] = to_row(l_sc[...])
        acc_out[0] = acc_sc[...]


def attend(bounds, q, kv, halves, state=None):
    rows = q.shape[0]
    _, n_blocks, block_rows, _ = kv.shape
    tile_blocks = TILE_KEYS // block_rows
    n_tiles = n_blocks // tile_blocks
    qrows = rows * GROUP

    phases = len(halves)

    def half_of(t):
        return halves[0] if phases == 1 else t // n_tiles

    def tile_of(t, b):
        phase = t // n_tiles
        first = b[2 * phase] // tile_blocks + t % n_tiles
        return jnp.minimum(first, b[2 * phase + 1] // tile_blocks)

    in_specs = [
        pl.BlockSpec((rows, GROUP * HEAD_DIM), lambda g, t, b: (0, g)),
        pl.BlockSpec(
            (None, tile_blocks, block_rows, HEAD_DIM),
            lambda g, t, b: (half_of(t), tile_of(t, b), 0, g),
        ),
        pl.BlockSpec(
            (None, tile_blocks, block_rows, HEAD_DIM),
            lambda g, t, b: (half_of(t), tile_of(t, b), 0, KV_HEADS + g),
        ),
    ]
    operands = [q, kv, kv]
    state_specs = [
        pl.BlockSpec((1, 1, qrows), lambda g, t, b: (g, 0, 0)),
        pl.BlockSpec((1, 1, qrows), lambda g, t, b: (g, 0, 0)),
        pl.BlockSpec((1, qrows, HEAD_DIM), lambda g, t, b: (g, 0, 0)),
    ]
    state_shapes = [
        jax.ShapeDtypeStruct((KV_HEADS, 1, qrows), jnp.float32),
        jax.ShapeDtypeStruct((KV_HEADS, 1, qrows), jnp.float32),
        jax.ShapeDtypeStruct((KV_HEADS, qrows, HEAD_DIM), jnp.float32),
    ]
    if state is not None:
        in_specs += state_specs
        operands += list(state)
    kernel = functools.partial(
        attend_kernel, carry_in=state is not None, tiles_per_phase=n_tiles
    )
    tile_flops = 4 * qrows * TILE_KEYS * HEAD_DIM
    cost = pl.CostEstimate(
        flops=KV_HEADS * n_tiles * phases * tile_flops,
        transcendentals=KV_HEADS * n_tiles * phases * qrows * TILE_KEYS,
        bytes_accessed=kv.size + q.size * 2 + KV_HEADS * qrows * HEAD_DIM * 8,
    )
    return pl.pallas_call(
        kernel,
        grid_spec=pltpu.PrefetchScalarGridSpec(
            num_scalar_prefetch=1,
            grid=(KV_HEADS, n_tiles * phases),
            in_specs=in_specs,
            out_specs=state_specs,
            scratch_shapes=[
                pltpu.VMEM((qrows, HEAD_DIM), jnp.bfloat16),
                pltpu.VMEM((qrows, 1), jnp.float32),
                pltpu.VMEM((qrows, 1), jnp.float32),
                pltpu.VMEM((qrows, HEAD_DIM), jnp.float32),
                pltpu.VMEM((TILE_KEYS, 2 * HEAD_DIM), jnp.bfloat16),
            ],
        ),
        out_shape=state_shapes,
        compiler_params=pltpu.CompilerParams(
            dimension_semantics=("arbitrary", "arbitrary"),
        ),
        cost_estimate=cost,
    )(bounds, *operands)


def split_halves(state, own_rows):
    mine, theirs = [], []
    for part in state:
        width = part.shape[-1] if part.shape[1] != 1 else 1
        shaped = part.reshape(KV_HEADS, GROUP, 2, own_rows, width)
        mine.append(shaped[:, :, 0])
        theirs.append(shaped[:, :, 1])
    return mine, theirs


def send_back(theirs, swap):
    run_max, run_sum, acc = theirs
    acc = lax.ppermute(acc.astype(jnp.bfloat16), "row", swap).astype(jnp.float32)
    stats = lax.ppermute(jnp.concatenate([run_max, run_sum], axis=-1), "row", swap)
    return [stats[..., 0:1], stats[..., 1:2], acc]


def finish(mine, theirs, gain):
    own_max, own_sum, own_acc = mine
    far_max, far_sum, far_acc = theirs
    top = jnp.maximum(own_max, far_max)
    own_factor = jnp.exp2((own_max - top) * EXP2_SCALE)
    far_factor = jnp.exp2((far_max - top) * EXP2_SCALE)
    total = own_sum * own_factor + far_sum * far_factor
    acc = own_acc * own_factor + far_acc * far_factor
    mixed = acc / total
    spread = jnp.sqrt(jnp.mean(mixed * mixed, axis=-1, keepdims=True) + 1e-06)
    normed = (mixed / spread * gain).astype(jnp.bfloat16)
    rows = normed.shape[2]
    return normed.transpose(2, 0, 1, 3).reshape(rows, KV_HEADS * GROUP * HEAD_DIM)


def per_device(queries, keys, values, gain, outer, inner):
    seq_index = lax.axis_index("outer") * inner + lax.axis_index("inner")
    last_index = outer * inner - 1
    own_rows = queries.shape[2]
    swap = [(0, 1), (1, 0)]
    partner_queries = lax.ppermute(queries, "row", swap)
    both_queries = jnp.concatenate([queries, partner_queries], axis=2)
    pair = jnp.concatenate([keys, values], axis=-1)
    blocks = lax.all_gather(pair[:, 0], "outer", axis=1, tiled=False)
    blocks = lax.all_gather(blocks, "inner", axis=2, tiled=False)
    blocks = blocks.reshape(2, outer * inner, own_rows, pair.shape[3])
    zero = jnp.int32(0)
    top = jnp.int32(last_index)

    early = attend(jnp.stack([zero, seq_index]), both_queries[0, 0], blocks, (0,))
    early_mine, early_theirs = split_halves(early, own_rows)
    early_back = send_back(early_theirs, swap)

    late = attend(
        jnp.stack([zero, top, seq_index, top]), both_queries[1, 0], blocks, (0, 1)
    )
    late_mine, late_theirs = split_halves(late, own_rows)
    late_back = send_back(late_theirs, swap)

    early_out = finish(early_mine, early_back, gain)
    late_out = finish(late_mine, late_back, gain)
    return jnp.stack([early_out, late_out]).reshape(2, 1, own_rows, KV_HEADS * GROUP * HEAD_DIM)


def solution(mesh):
    seq_count, row_count = mesh.devices.shape
    outer = math.gcd(seq_count, 4)
    inner = seq_count // outer
    split = Mesh(mesh.devices.reshape(outer, inner, row_count), ("outer", "inner", "row"))
    spec = P(None, ("outer", "inner"), "row", None)
    return jax.shard_map(
        functools.partial(per_device, outer=outer, inner=inner),
        mesh=split,
        in_specs=(spec, spec, spec, P()),
        out_specs=spec,
        check_vma=False,
    )
```

```python
import functools
import math

import jax
import jax.numpy as jnp
from jax import lax
from jax.experimental import pallas as pl
from jax.experimental.pallas import tpu as pltpu
from jax.sharding import Mesh, PartitionSpec as P

KV_HEADS = 4
GROUP = 6
HEAD_DIM = 128
TILE_KEYS = 1024

lowest_score = -1e30
EXP2_SCALE = math.log2(math.e) / math.sqrt(HEAD_DIM)


def to_row(column):
    return jnp.transpose(jnp.broadcast_to(column, (column.shape[0], HEAD_DIM)))[0:1, :]


def from_row(row):
    return jnp.transpose(jnp.broadcast_to(row, (HEAD_DIM, row.shape[1])))[:, 0:1]


def attend_kernel(bounds_ref, q_ref, k_ref, v_ref, *rest, carry_in, tiles_per_phase):
    if carry_in:
        m_in, l_in, acc_in = rest[:3]
        rest = rest[3:]
    m_out, l_out, acc_out = rest[:3]
    q_sc, m_sc, l_sc, acc_sc, vals_sc = rest[3:]

    t = pl.program_id(1)
    last = pl.num_programs(1) - 1
    tile_blocks, block_rows, _ = k_ref.shape
    phase = t // tiles_per_phase
    lo = bounds_ref[2 * phase]
    hi = bounds_ref[2 * phase + 1]
    tile = lo // tile_blocks + t % tiles_per_phase
    first_block = tile * tile_blocks

    @pl.when(t == 0)
    def _init():
        vals_sc[:, HEAD_DIM:] = jnp.ones((vals_sc.shape[0], HEAD_DIM), jnp.bfloat16)
        q_sc[...] = jnp.concatenate(
            [q_ref[:, j * HEAD_DIM:(j + 1) * HEAD_DIM] for j in range(GROUP)], axis=0
        )
        if carry_in:
            m_sc[...] = from_row(m_in[0])
            l_sc[...] = from_row(l_in[0])
            acc_sc[...] = acc_in[0]
        else:
            m_sc[...] = jnp.full(m_sc.shape, lowest_score, jnp.float32)
            l_sc[...] = jnp.zeros(l_sc.shape, jnp.float32)
            acc_sc[...] = jnp.zeros(acc_sc.shape, jnp.float32)

    def step(masked):
        keys = k_ref[...].reshape(tile_blocks * block_rows, HEAD_DIM)
        vals_sc[:, :HEAD_DIM] = v_ref[...].reshape(tile_blocks * block_rows, HEAD_DIM)
        vals = vals_sc[...]
        half = q_sc.shape[0] // 2
        bias = None
        if masked:
            key_block = first_block + lax.broadcasted_iota(
                jnp.int32, (1, tile_blocks * block_rows), 1
            ) // block_rows
            visible = (key_block >= lo) & (key_block <= hi)
            bias = jnp.where(visible, 0.0, -jnp.inf).astype(jnp.float32)
        for part in range(2):
            rows_here = pl.ds(part * half, half)
            half_step(bias, keys, vals, rows_here)

    def half_step(bias, keys, vals, rows_here):
        scores = lax.dot_general(
            q_sc[rows_here], keys, (((1,), (1,)), ((), ())), preferred_element_type=jnp.float32
        )
        if bias is not None:
            scores = scores + bias
        running_max = m_sc[rows_here]
        new_max = jnp.maximum(running_max, jnp.max(scores, axis=1, keepdims=True))
        raw_weights = jnp.exp2((scores - new_max) * EXP2_SCALE)
        factor = jnp.exp2((running_max - new_max) * EXP2_SCALE)
        mixed = jnp.dot(
            raw_weights.astype(jnp.bfloat16), vals, preferred_element_type=jnp.float32
        )
        l_sc[rows_here] = l_sc[rows_here] * factor + mixed[:, HEAD_DIM:HEAD_DIM + 1]
        acc_sc[rows_here] = acc_sc[rows_here] * factor + mixed[:, :HEAD_DIM]
        m_sc[rows_here] = new_max

    active = tile <= hi // tile_blocks
    edge = (first_block < lo) | (first_block + tile_blocks - 1 > hi)

    @pl.when(active & edge)
    def _edge_step():
        step(True)

    @pl.when(active & jnp.logical_not(edge))
    def _inner_step():
        step(False)

    @pl.when(t == last)
    def _done():
        m_out[0] = to_row(m_sc[...])
        l_out[0] = to_row(l_sc[...])
        acc_out[0] = acc_sc[...]


def attend(bounds, q, kv, halves, state=None):
    rows = q.shape[0]
    _, n_blocks, block_rows, _ = kv.shape
    tile_blocks = TILE_KEYS // block_rows
    n_tiles = n_blocks // tile_blocks
    qrows = rows * GROUP

    phases = len(halves)

    def half_of(t):
        return halves[0] if phases == 1 else t // n_tiles

    def tile_of(t, b):
        phase = t // n_tiles
        first = b[2 * phase] // tile_blocks + t % n_tiles
        return jnp.minimum(first, b[2 * phase + 1] // tile_blocks)

    in_specs = [
        pl.BlockSpec((rows, GROUP * HEAD_DIM), lambda g, t, b: (0, g)),
        pl.BlockSpec(
            (None, tile_blocks, block_rows, HEAD_DIM),
            lambda g, t, b: (half_of(t), tile_of(t, b), 0, g),
        ),
        pl.BlockSpec(
            (None, tile_blocks, block_rows, HEAD_DIM),
            lambda g, t, b: (half_of(t), tile_of(t, b), 0, KV_HEADS + g),
        ),
    ]
    operands = [q, kv, kv]
    state_specs = [
        pl.BlockSpec((1, 1, qrows), lambda g, t, b: (g, 0, 0)),
        pl.BlockSpec((1, 1, qrows), lambda g, t, b: (g, 0, 0)),
        pl.BlockSpec((1, qrows, HEAD_DIM), lambda g, t, b: (g, 0, 0)),
    ]
    state_shapes = [
        jax.ShapeDtypeStruct((KV_HEADS, 1, qrows), jnp.float32),
        jax.ShapeDtypeStruct((KV_HEADS, 1, qrows), jnp.float32),
        jax.ShapeDtypeStruct((KV_HEADS, qrows, HEAD_DIM), jnp.float32),
    ]
    if state is not None:
        in_specs += state_specs
        operands += list(state)
    kernel = functools.partial(
        attend_kernel, carry_in=state is not None, tiles_per_phase=n_tiles
    )
    tile_flops = 4 * qrows * TILE_KEYS * HEAD_DIM
    cost = pl.CostEstimate(
        flops=KV_HEADS * n_tiles * phases * tile_flops,
        transcendentals=KV_HEADS * n_tiles * phases * qrows * TILE_KEYS,
        bytes_accessed=kv.size + q.size * 2 + KV_HEADS * qrows * HEAD_DIM * 8,
    )
    return pl.pallas_call(
        kernel,
        grid_spec=pltpu.PrefetchScalarGridSpec(
            num_scalar_prefetch=1,
            grid=(KV_HEADS, n_tiles * phases),
            in_specs=in_specs,
            out_specs=state_specs,
            scratch_shapes=[
                pltpu.VMEM((qrows, HEAD_DIM), jnp.bfloat16),
                pltpu.VMEM((qrows, 1), jnp.float32),
                pltpu.VMEM((qrows, 1), jnp.float32),
                pltpu.VMEM((qrows, HEAD_DIM), jnp.float32),
                pltpu.VMEM((TILE_KEYS, 2 * HEAD_DIM), jnp.bfloat16),
            ],
        ),
        out_shape=state_shapes,
        compiler_params=pltpu.CompilerParams(
            dimension_semantics=("arbitrary", "arbitrary"),
        ),
        cost_estimate=cost,
    )(bounds, *operands)


def split_halves(state, own_rows):
    mine, theirs = [], []
    for part in state:
        width = part.shape[-1] if part.shape[1] != 1 else 1
        shaped = part.reshape(KV_HEADS, GROUP, 2, own_rows, width)
        mine.append(shaped[:, :, 0])
        theirs.append(shaped[:, :, 1])
    return mine, theirs


def send_back(theirs, swap):
    run_max, run_sum, acc = theirs
    acc = lax.ppermute(acc.astype(jnp.bfloat16), "row", swap).astype(jnp.float32)
    stats = lax.ppermute(jnp.concatenate([run_max, run_sum], axis=-1), "row", swap)
    return [stats[..., 0:1], stats[..., 1:2], acc]


def finish(mine, theirs, gain):
    own_max, own_sum, own_acc = mine
    far_max, far_sum, far_acc = theirs
    top = jnp.maximum(own_max, far_max)
    own_factor = jnp.exp2((own_max - top) * EXP2_SCALE)
    far_factor = jnp.exp2((far_max - top) * EXP2_SCALE)
    total = own_sum * own_factor + far_sum * far_factor
    acc = own_acc * own_factor + far_acc * far_factor
    mixed = acc / total
    spread = jnp.sqrt(jnp.mean(mixed * mixed, axis=-1, keepdims=True) + 1e-06)
    normed = (mixed / spread * gain).astype(jnp.bfloat16)
    rows = normed.shape[2]
    return normed.transpose(2, 0, 1, 3).reshape(rows, KV_HEADS * GROUP * HEAD_DIM)


def per_device(queries, keys, values, gain, outer, inner):
    seq_index = lax.axis_index("outer") * inner + lax.axis_index("inner")
    last_index = outer * inner - 1
    own_rows = queries.shape[2]
    swap = [(0, 1), (1, 0)]
    partner_queries = lax.ppermute(queries, "row", swap)
    both_queries = jnp.concatenate([queries, partner_queries], axis=2)
    pair = jnp.concatenate([keys, values], axis=-1)
    blocks = lax.all_gather(pair[:, 0], "outer", axis=1, tiled=False)
    blocks = lax.all_gather(blocks, "inner", axis=2, tiled=False)
    blocks = blocks.reshape(2, outer * inner, own_rows, pair.shape[3])
    zero = jnp.int32(0)
    top = jnp.int32(last_index)

    early = attend(jnp.stack([zero, seq_index]), both_queries[0, 0], blocks, (0,))
    early_mine, early_theirs = split_halves(early, own_rows)
    early_back = send_back(early_theirs, swap)
    late_bounds = jnp.stack([zero, top, seq_index, top])
    early_back, late_bounds = lax.optimization_barrier((early_back, late_bounds))

    late = attend(late_bounds, both_queries[1, 0], blocks, (0, 1))
    late_mine, late_theirs = split_halves(late, own_rows)
    late_back = send_back(late_theirs, swap)

    early_out = finish(early_mine, early_back, gain)
    late_out = finish(late_mine, late_back, gain)
    return jnp.stack([early_out, late_out]).reshape(2, 1, own_rows, KV_HEADS * GROUP * HEAD_DIM)


def solution(mesh):
    seq_count, row_count = mesh.devices.shape
    outer = math.gcd(seq_count, 4)
    inner = seq_count // outer
    split = Mesh(mesh.devices.reshape(outer, inner, row_count), ("outer", "inner", "row"))
    spec = P(None, ("outer", "inner"), "row", None)
    return jax.shard_map(
        functools.partial(per_device, outer=outer, inner=inner),
        mesh=split,
        in_specs=(spec, spec, spec, P()),
        out_specs=spec,
        check_vma=False,
    )
```

```python
import functools
import math

import jax
import jax.numpy as jnp
from jax import lax
from jax.experimental import pallas as pl
from jax.experimental.pallas import tpu as pltpu
from jax.sharding import Mesh, PartitionSpec as P

KV_HEADS = 4
GROUP = 6
HEAD_DIM = 128
TILE_KEYS = 1024

lowest_score = -1e30
EXP2_SCALE = math.log2(math.e) / math.sqrt(HEAD_DIM)


def to_row(column):
    return jnp.transpose(jnp.broadcast_to(column, (column.shape[0], HEAD_DIM)))[0:1, :]


def from_row(row):
    return jnp.transpose(jnp.broadcast_to(row, (HEAD_DIM, row.shape[1])))[:, 0:1]


def attend_kernel(bounds_ref, q_ref, k_ref, v_ref, *rest, carry_in, tiles_per_phase):
    if carry_in:
        m_in, l_in, acc_in = rest[:3]
        rest = rest[3:]
    m_out, l_out, acc_out = rest[:3]
    q_sc, m_sc, l_sc, acc_sc, vals_sc = rest[3:]

    t = pl.program_id(1)
    last = pl.num_programs(1) - 1
    tile_blocks, block_rows, _ = k_ref.shape
    phase = t // tiles_per_phase
    lo = bounds_ref[2 * phase]
    hi = bounds_ref[2 * phase + 1]
    tile = lo // tile_blocks + t % tiles_per_phase
    first_block = tile * tile_blocks

    @pl.when(t == 0)
    def _init():
        vals_sc[:, HEAD_DIM:] = jnp.ones((vals_sc.shape[0], HEAD_DIM), jnp.bfloat16)
        q_sc[...] = jnp.concatenate(
            [q_ref[:, j * HEAD_DIM:(j + 1) * HEAD_DIM] for j in range(GROUP)], axis=0
        )
        if carry_in:
            m_sc[...] = from_row(m_in[0])
            l_sc[...] = from_row(l_in[0])
            acc_sc[...] = acc_in[0]
        else:
            m_sc[...] = jnp.full(m_sc.shape, lowest_score, jnp.float32)
            l_sc[...] = jnp.zeros(l_sc.shape, jnp.float32)
            acc_sc[...] = jnp.zeros(acc_sc.shape, jnp.float32)

    def step(masked):
        keys = k_ref[...].reshape(tile_blocks * block_rows, HEAD_DIM)
        vals_sc[:, :HEAD_DIM] = v_ref[...].reshape(tile_blocks * block_rows, HEAD_DIM)
        vals = vals_sc[...]
        half = q_sc.shape[0] // 2
        bias = None
        if masked:
            key_block = first_block + lax.broadcasted_iota(
                jnp.int32, (1, tile_blocks * block_rows), 1
            ) // block_rows
            visible = (key_block >= lo) & (key_block <= hi)
            bias = jnp.where(visible, 0.0, -jnp.inf).astype(jnp.float32)
        for part in range(2):
            rows_here = pl.ds(part * half, half)
            half_step(bias, keys, vals, rows_here)

    def half_step(bias, keys, vals, rows_here):
        scores = lax.dot_general(
            q_sc[rows_here], keys, (((1,), (1,)), ((), ())), preferred_element_type=jnp.float32
        )
        if bias is not None:
            scores = scores + bias
        running_max = m_sc[rows_here]
        new_max = jnp.maximum(running_max, jnp.max(scores, axis=1, keepdims=True))
        raw_weights = jnp.exp2((scores - new_max) * EXP2_SCALE)
        factor = jnp.exp2((running_max - new_max) * EXP2_SCALE)
        mixed = jnp.dot(
            raw_weights.astype(jnp.bfloat16), vals, preferred_element_type=jnp.float32
        )
        l_sc[rows_here] = l_sc[rows_here] * factor + mixed[:, HEAD_DIM:HEAD_DIM + 1]
        acc_sc[rows_here] = acc_sc[rows_here] * factor + mixed[:, :HEAD_DIM]
        m_sc[rows_here] = new_max

    active = tile <= hi // tile_blocks
    edge = (first_block < lo) | (first_block + tile_blocks - 1 > hi)

    @pl.when(active & edge)
    def _edge_step():
        step(True)

    @pl.when(active & jnp.logical_not(edge))
    def _inner_step():
        step(False)

    @pl.when(t == last)
    def _done():
        m_out[0] = to_row(m_sc[...])
        l_out[0] = to_row(l_sc[...])
        acc_out[0] = acc_sc[...]


def attend(bounds, q, kv, halves, state=None):
    rows = q.shape[0]
    _, n_blocks, block_rows, _ = kv.shape
    tile_blocks = TILE_KEYS // block_rows
    n_tiles = n_blocks // tile_blocks
    qrows = rows * GROUP

    phases = len(halves)

    def half_of(t):
        return halves[0] if phases == 1 else t // n_tiles

    def tile_of(t, b):
        phase = t // n_tiles
        first = b[2 * phase] // tile_blocks + t % n_tiles
        return jnp.minimum(first, b[2 * phase + 1] // tile_blocks)

    in_specs = [
        pl.BlockSpec((rows, GROUP * HEAD_DIM), lambda g, t, b: (0, g)),
        pl.BlockSpec(
            (None, tile_blocks, block_rows, HEAD_DIM),
            lambda g, t, b: (half_of(t), tile_of(t, b), 0, g),
        ),
        pl.BlockSpec(
            (None, tile_blocks, block_rows, HEAD_DIM),
            lambda g, t, b: (half_of(t), tile_of(t, b), 0, KV_HEADS + g),
        ),
    ]
    operands = [q, kv, kv]
    state_specs = [
        pl.BlockSpec((1, 1, qrows), lambda g, t, b: (g, 0, 0)),
        pl.BlockSpec((1, 1, qrows), lambda g, t, b: (g, 0, 0)),
        pl.BlockSpec((1, qrows, HEAD_DIM), lambda g, t, b: (g, 0, 0)),
    ]
    state_shapes = [
        jax.ShapeDtypeStruct((KV_HEADS, 1, qrows), jnp.float32),
        jax.ShapeDtypeStruct((KV_HEADS, 1, qrows), jnp.float32),
        jax.ShapeDtypeStruct((KV_HEADS, qrows, HEAD_DIM), jnp.float32),
    ]
    if state is not None:
        in_specs += state_specs
        operands += list(state)
    kernel = functools.partial(
        attend_kernel, carry_in=state is not None, tiles_per_phase=n_tiles
    )
    tile_flops = 4 * qrows * TILE_KEYS * HEAD_DIM
    cost = pl.CostEstimate(
        flops=KV_HEADS * n_tiles * phases * tile_flops,
        transcendentals=KV_HEADS * n_tiles * phases * qrows * TILE_KEYS,
        bytes_accessed=kv.size + q.size * 2 + KV_HEADS * qrows * HEAD_DIM * 8,
    )
    return pl.pallas_call(
        kernel,
        grid_spec=pltpu.PrefetchScalarGridSpec(
            num_scalar_prefetch=1,
            grid=(KV_HEADS, n_tiles * phases),
            in_specs=in_specs,
            out_specs=state_specs,
            scratch_shapes=[
                pltpu.VMEM((qrows, HEAD_DIM), jnp.bfloat16),
                pltpu.VMEM((qrows, 1), jnp.float32),
                pltpu.VMEM((qrows, 1), jnp.float32),
                pltpu.VMEM((qrows, HEAD_DIM), jnp.float32),
                pltpu.VMEM((TILE_KEYS, 2 * HEAD_DIM), jnp.bfloat16),
            ],
        ),
        out_shape=state_shapes,
        compiler_params=pltpu.CompilerParams(
            dimension_semantics=("arbitrary", "arbitrary"),
        ),
        cost_estimate=cost,
    )(bounds, *operands)


def split_halves(state, own_rows):
    mine, theirs = [], []
    for part in state:
        width = part.shape[-1] if part.shape[1] != 1 else 1
        shaped = part.reshape(KV_HEADS, GROUP, 2, own_rows, width)
        mine.append(shaped[:, :, 0])
        theirs.append(shaped[:, :, 1])
    return mine, theirs


def send_back(theirs, swap):
    run_max, run_sum, acc = theirs
    acc = lax.ppermute(acc.astype(jnp.bfloat16), "row", swap).astype(jnp.float32)
    stats = lax.ppermute(jnp.concatenate([run_max, run_sum], axis=-1), "row", swap)
    return [stats[..., 0:1], stats[..., 1:2], acc]


def finish(mine, theirs, gain):
    own_max, own_sum, own_acc = mine
    far_max, far_sum, far_acc = theirs
    top = jnp.maximum(own_max, far_max)
    own_factor = jnp.exp2((own_max - top) * EXP2_SCALE)
    far_factor = jnp.exp2((far_max - top) * EXP2_SCALE)
    total = own_sum * own_factor + far_sum * far_factor
    acc = own_acc * own_factor + far_acc * far_factor
    mixed = acc / total
    spread = jnp.sqrt(jnp.mean(mixed * mixed, axis=-1, keepdims=True) + 1e-06)
    normed = (mixed / spread * gain).astype(jnp.bfloat16)
    rows = normed.shape[2]
    return normed.transpose(2, 0, 1, 3).reshape(rows, KV_HEADS * GROUP * HEAD_DIM)


def per_device(queries, keys, values, gain, outer, inner):
    seq_index = lax.axis_index("outer") * inner + lax.axis_index("inner")
    last_index = outer * inner - 1
    own_rows = queries.shape[2]
    swap = [(0, 1), (1, 0)]
    partner_queries = lax.ppermute(queries, "row", swap)
    both_queries = jnp.concatenate([queries, partner_queries], axis=2)
    pair = jnp.concatenate([keys, values], axis=-1)
    blocks = lax.all_gather(pair[:, 0], "outer", axis=1, tiled=False)
    blocks = lax.all_gather(blocks, "inner", axis=2, tiled=False)
    blocks = blocks.reshape(2, outer * inner, own_rows, pair.shape[3])
    zero = jnp.int32(0)
    top = jnp.int32(last_index)

    early = attend(jnp.stack([zero, seq_index]), both_queries[0, 0], blocks, (0,))
    early_mine, early_theirs = split_halves(early, own_rows)

    late = attend(
        jnp.stack([zero, top, seq_index, top]), both_queries[1, 0], blocks, (0, 1)
    )
    late_mine, late_theirs = split_halves(late, own_rows)
    both_back = send_back([jnp.stack(pair) for pair in zip(early_theirs, late_theirs)], swap)
    early_back = [x[0] for x in both_back]
    late_back = [x[1] for x in both_back]

    early_out = finish(early_mine, early_back, gain)
    late_out = finish(late_mine, late_back, gain)
    return jnp.stack([early_out, late_out]).reshape(2, 1, own_rows, KV_HEADS * GROUP * HEAD_DIM)


def solution(mesh):
    seq_count, row_count = mesh.devices.shape
    outer = math.gcd(seq_count, 4)
    inner = seq_count // outer
    split = Mesh(mesh.devices.reshape(outer, inner, row_count), ("outer", "inner", "row"))
    spec = P(None, ("outer", "inner"), "row", None)
    return jax.shard_map(
        functools.partial(per_device, outer=outer, inner=inner),
        mesh=split,
        in_specs=(spec, spec, spec, P()),
        out_specs=spec,
        check_vma=False,
    )
```

```python
import functools
import math

import jax
import jax.numpy as jnp
from jax import lax
from jax.experimental import pallas as pl
from jax.experimental.pallas import tpu as pltpu
from jax.sharding import Mesh, PartitionSpec as P

KV_HEADS = 4
GROUP = 6
HEAD_DIM = 128
TILE_KEYS = 1024

lowest_score = -1e30
EXP2_SCALE = math.log2(math.e) / math.sqrt(HEAD_DIM)


def to_row(column):
    return jnp.transpose(jnp.broadcast_to(column, (column.shape[0], HEAD_DIM)))[0:1, :]


def from_row(row):
    return jnp.transpose(jnp.broadcast_to(row, (HEAD_DIM, row.shape[1])))[:, 0:1]


def attend_kernel(bounds_ref, q_ref, k_ref, v_ref, *rest, carry_in, tiles_per_phase):
    if carry_in:
        m_in, l_in, acc_in = rest[:3]
        rest = rest[3:]
    m_out, l_out, acc_out = rest[:3]
    q_sc, m_sc, l_sc, acc_sc, vals_sc = rest[3:]

    t = pl.program_id(1)
    last = pl.num_programs(1) - 1
    tile_blocks, block_rows, _ = k_ref.shape
    phase = t // tiles_per_phase
    lo = bounds_ref[2 * phase]
    hi = bounds_ref[2 * phase + 1]
    tile = lo // tile_blocks + t % tiles_per_phase
    first_block = tile * tile_blocks

    @pl.when(t == 0)
    def _init():
        vals_sc[:, HEAD_DIM:] = jnp.ones((vals_sc.shape[0], HEAD_DIM), jnp.bfloat16)
        q_sc[...] = jnp.concatenate(
            [q_ref[:, j * HEAD_DIM:(j + 1) * HEAD_DIM] for j in range(GROUP)], axis=0
        )
        if carry_in:
            m_sc[...] = from_row(m_in[0])
            l_sc[...] = from_row(l_in[0])
            acc_sc[...] = acc_in[0]
        else:
            m_sc[...] = jnp.full(m_sc.shape, lowest_score, jnp.float32)
            l_sc[...] = jnp.zeros(l_sc.shape, jnp.float32)
            acc_sc[...] = jnp.zeros(acc_sc.shape, jnp.float32)

    def step(masked):
        keys = k_ref[...].reshape(tile_blocks * block_rows, HEAD_DIM)
        vals_sc[:, :HEAD_DIM] = v_ref[...].reshape(tile_blocks * block_rows, HEAD_DIM)
        vals = vals_sc[...]
        half = q_sc.shape[0] // 2
        bias = None
        if masked:
            key_block = first_block + lax.broadcasted_iota(
                jnp.int32, (1, tile_blocks * block_rows), 1
            ) // block_rows
            visible = (key_block >= lo) & (key_block <= hi)
            bias = jnp.where(visible, 0.0, -jnp.inf).astype(jnp.float32)
        for part in range(2):
            rows_here = pl.ds(part * half, half)
            half_step(bias, keys, vals, rows_here)

    def half_step(bias, keys, vals, rows_here):
        scores = lax.dot_general(
            q_sc[rows_here], keys, (((1,), (1,)), ((), ())), preferred_element_type=jnp.float32
        )
        if bias is not None:
            scores = scores + bias
        running_max = m_sc[rows_here]
        new_max = jnp.maximum(running_max, jnp.max(scores, axis=1, keepdims=True))
        raw_weights = jnp.exp2((scores - new_max) * EXP2_SCALE)
        factor = jnp.exp2((running_max - new_max) * EXP2_SCALE)
        mixed = jnp.dot(
            raw_weights.astype(jnp.bfloat16), vals, preferred_element_type=jnp.float32
        )
        l_sc[rows_here] = l_sc[rows_here] * factor + mixed[:, HEAD_DIM:HEAD_DIM + 1]
        acc_sc[rows_here] = acc_sc[rows_here] * factor + mixed[:, :HEAD_DIM]
        m_sc[rows_here] = new_max

    active = tile <= hi // tile_blocks
    edge = (first_block < lo) | (first_block + tile_blocks - 1 > hi)

    @pl.when(active & edge)
    def _edge_step():
        step(True)

    @pl.when(active & jnp.logical_not(edge))
    def _inner_step():
        step(False)

    @pl.when(t == last)
    def _done():
        m_out[0] = to_row(m_sc[...])
        l_out[0] = to_row(l_sc[...])
        acc_out[0] = acc_sc[...]


def attend(bounds, q, kv, halves, state=None):
    rows = q.shape[0]
    _, n_blocks, block_rows, _ = kv.shape
    tile_blocks = TILE_KEYS // block_rows
    n_tiles = n_blocks // tile_blocks
    qrows = rows * GROUP

    phases = len(halves)

    def half_of(t):
        return halves[0] if phases == 1 else t // n_tiles

    def tile_of(t, b):
        phase = t // n_tiles
        first = b[2 * phase] // tile_blocks + t % n_tiles
        return jnp.minimum(first, b[2 * phase + 1] // tile_blocks)

    in_specs = [
        pl.BlockSpec((rows, GROUP * HEAD_DIM), lambda g, t, b: (0, g)),
        pl.BlockSpec(
            (None, tile_blocks, block_rows, HEAD_DIM),
            lambda g, t, b: (half_of(t), tile_of(t, b), 0, g),
        ),
        pl.BlockSpec(
            (None, tile_blocks, block_rows, HEAD_DIM),
            lambda g, t, b: (half_of(t), tile_of(t, b), 0, KV_HEADS + g),
        ),
    ]
    operands = [q, kv, kv]
    state_specs = [
        pl.BlockSpec((1, 1, qrows), lambda g, t, b: (g, 0, 0)),
        pl.BlockSpec((1, 1, qrows), lambda g, t, b: (g, 0, 0)),
        pl.BlockSpec((1, qrows, HEAD_DIM), lambda g, t, b: (g, 0, 0)),
    ]
    state_shapes = [
        jax.ShapeDtypeStruct((KV_HEADS, 1, qrows), jnp.float32),
        jax.ShapeDtypeStruct((KV_HEADS, 1, qrows), jnp.float32),
        jax.ShapeDtypeStruct((KV_HEADS, qrows, HEAD_DIM), jnp.float32),
    ]
    if state is not None:
        in_specs += state_specs
        operands += list(state)
    kernel = functools.partial(
        attend_kernel, carry_in=state is not None, tiles_per_phase=n_tiles
    )
    tile_flops = 4 * qrows * TILE_KEYS * HEAD_DIM
    cost = pl.CostEstimate(
        flops=KV_HEADS * n_tiles * phases * tile_flops,
        transcendentals=KV_HEADS * n_tiles * phases * qrows * TILE_KEYS,
        bytes_accessed=kv.size + q.size * 2 + KV_HEADS * qrows * HEAD_DIM * 8,
    )
    return pl.pallas_call(
        kernel,
        grid_spec=pltpu.PrefetchScalarGridSpec(
            num_scalar_prefetch=1,
            grid=(KV_HEADS, n_tiles * phases),
            in_specs=in_specs,
            out_specs=state_specs,
            scratch_shapes=[
                pltpu.VMEM((qrows, HEAD_DIM), jnp.bfloat16),
                pltpu.VMEM((qrows, 1), jnp.float32),
                pltpu.VMEM((qrows, 1), jnp.float32),
                pltpu.VMEM((qrows, HEAD_DIM), jnp.float32),
                pltpu.VMEM((TILE_KEYS, 2 * HEAD_DIM), jnp.bfloat16),
            ],
        ),
        out_shape=state_shapes,
        compiler_params=pltpu.CompilerParams(
            dimension_semantics=("arbitrary", "arbitrary"),
        ),
        cost_estimate=cost,
    )(bounds, *operands)


def split_halves(state, own_rows):
    mine, theirs = [], []
    for part in state:
        width = part.shape[-1] if part.shape[1] != 1 else 1
        shaped = part.reshape(KV_HEADS, GROUP, 2, own_rows, width)
        mine.append(shaped[:, :, 0])
        theirs.append(shaped[:, :, 1])
    return mine, theirs


def send_back(theirs, swap):
    run_max, run_sum, acc = theirs
    acc = lax.ppermute(acc.astype(jnp.bfloat16), "row", swap).astype(jnp.float32)
    stats = lax.ppermute(jnp.concatenate([run_max, run_sum], axis=-1), "row", swap)
    return [stats[..., 0:1], stats[..., 1:2], acc]


def finish(mine, theirs, gain):
    own_max, own_sum, own_acc = mine
    far_max, far_sum, far_acc = theirs
    top = jnp.maximum(own_max, far_max)
    own_factor = jnp.exp2((own_max - top) * EXP2_SCALE)
    far_factor = jnp.exp2((far_max - top) * EXP2_SCALE)
    total = own_sum * own_factor + far_sum * far_factor
    acc = own_acc * own_factor + far_acc * far_factor
    mixed = acc / total
    spread = jnp.sqrt(jnp.mean(mixed * mixed, axis=-1, keepdims=True) + 1e-06)
    normed = (mixed / spread * gain).astype(jnp.bfloat16)
    halves, rows = normed.shape[0], normed.shape[3]
    return normed.transpose(0, 3, 1, 2, 4).reshape(halves, 1, rows, KV_HEADS * GROUP * HEAD_DIM)


def per_device(queries, keys, values, gain, outer, inner):
    seq_index = lax.axis_index("outer") * inner + lax.axis_index("inner")
    last_index = outer * inner - 1
    own_rows = queries.shape[2]
    swap = [(0, 1), (1, 0)]
    partner_queries = lax.ppermute(queries, "row", swap)
    both_queries = jnp.concatenate([queries, partner_queries], axis=2)
    pair = jnp.concatenate([keys, values], axis=-1)
    blocks = lax.all_gather(pair[:, 0], "outer", axis=1, tiled=False)
    blocks = lax.all_gather(blocks, "inner", axis=2, tiled=False)
    blocks = blocks.reshape(2, outer * inner, own_rows, pair.shape[3])
    zero = jnp.int32(0)
    top = jnp.int32(last_index)

    early = attend(jnp.stack([zero, seq_index]), both_queries[0, 0], blocks, (0,))
    early_mine, early_theirs = split_halves(early, own_rows)

    late = attend(
        jnp.stack([zero, top, seq_index, top]), both_queries[1, 0], blocks, (0, 1)
    )
    late_mine, late_theirs = split_halves(late, own_rows)
    both_back = send_back([jnp.stack(pair) for pair in zip(early_theirs, late_theirs)], swap)

    both_mine = [jnp.stack(pair) for pair in zip(early_mine, late_mine)]
    return finish(both_mine, both_back, gain)


def solution(mesh):
    seq_count, row_count = mesh.devices.shape
    outer = math.gcd(seq_count, 4)
    inner = seq_count // outer
    split = Mesh(mesh.devices.reshape(outer, inner, row_count), ("outer", "inner", "row"))
    spec = P(None, ("outer", "inner"), "row", None)
    return jax.shard_map(
        functools.partial(per_device, outer=outer, inner=inner),
        mesh=split,
        in_specs=(spec, spec, spec, P()),
        out_specs=spec,
        check_vma=False,
    )
```

```python
import functools
import math

import jax
import jax.numpy as jnp
from jax import lax
from jax.experimental import pallas as pl
from jax.experimental.pallas import tpu as pltpu
from jax.sharding import Mesh, PartitionSpec as P

KV_HEADS = 4
GROUP = 6
HEAD_DIM = 128
TILE_KEYS = 1024

lowest_score = -1e30
EXP2_SCALE = math.log2(math.e) / math.sqrt(HEAD_DIM)


def to_row(column):
    return jnp.transpose(jnp.broadcast_to(column, (column.shape[0], HEAD_DIM)))[0:1, :]


def from_row(row):
    return jnp.transpose(jnp.broadcast_to(row, (HEAD_DIM, row.shape[1])))[:, 0:1]


def attend_kernel(bounds_ref, q_ref, k_ref, v_ref, *rest, carry_in, tiles_per_phase):
    if carry_in:
        m_in, l_in, acc_in = rest[:3]
        rest = rest[3:]
    m_out, l_out, acc_out, far_out = rest[:4]
    q_sc, m_sc, l_sc, acc_sc, vals_sc = rest[4:]

    t = pl.program_id(1)
    last = pl.num_programs(1) - 1
    tile_blocks, block_rows, _ = k_ref.shape
    phase = t // tiles_per_phase
    lo = bounds_ref[2 * phase]
    hi = bounds_ref[2 * phase + 1]
    tile = lo // tile_blocks + t % tiles_per_phase
    first_block = tile * tile_blocks

    @pl.when(t == 0)
    def _init():
        vals_sc[:, HEAD_DIM:] = jnp.ones((vals_sc.shape[0], HEAD_DIM), jnp.bfloat16)
        q_sc[...] = jnp.concatenate(
            [q_ref[:, j * HEAD_DIM:(j + 1) * HEAD_DIM] for j in range(GROUP)], axis=0
        )
        if carry_in:
            m_sc[...] = from_row(m_in[0])
            l_sc[...] = from_row(l_in[0])
            acc_sc[...] = acc_in[0]
        else:
            m_sc[...] = jnp.full(m_sc.shape, lowest_score, jnp.float32)
            l_sc[...] = jnp.zeros(l_sc.shape, jnp.float32)
            acc_sc[...] = jnp.zeros(acc_sc.shape, jnp.float32)

    def step(masked):
        keys = k_ref[...].reshape(tile_blocks * block_rows, HEAD_DIM)
        vals_sc[:, :HEAD_DIM] = v_ref[...].reshape(tile_blocks * block_rows, HEAD_DIM)
        vals = vals_sc[...]
        half = q_sc.shape[0] // 2
        bias = None
        if masked:
            key_block = first_block + lax.broadcasted_iota(
                jnp.int32, (1, tile_blocks * block_rows), 1
            ) // block_rows
            visible = (key_block >= lo) & (key_block <= hi)
            bias = jnp.where(visible, 0.0, -jnp.inf).astype(jnp.float32)
        for part in range(2):
            rows_here = pl.ds(part * half, half)
            half_step(bias, keys, vals, rows_here)

    def half_step(bias, keys, vals, rows_here):
        scores = lax.dot_general(
            q_sc[rows_here], keys, (((1,), (1,)), ((), ())), preferred_element_type=jnp.float32
        )
        if bias is not None:
            scores = scores + bias
        running_max = m_sc[rows_here]
        new_max = jnp.maximum(running_max, jnp.max(scores, axis=1, keepdims=True))
        raw_weights = jnp.exp2((scores - new_max) * EXP2_SCALE)
        factor = jnp.exp2((running_max - new_max) * EXP2_SCALE)
        mixed = jnp.dot(
            raw_weights.astype(jnp.bfloat16), vals, preferred_element_type=jnp.float32
        )
        l_sc[rows_here] = l_sc[rows_here] * factor + mixed[:, HEAD_DIM:HEAD_DIM + 1]
        acc_sc[rows_here] = acc_sc[rows_here] * factor + mixed[:, :HEAD_DIM]
        m_sc[rows_here] = new_max

    active = tile <= hi // tile_blocks
    edge = (first_block < lo) | (first_block + tile_blocks - 1 > hi)

    @pl.when(active & edge)
    def _edge_step():
        step(True)

    @pl.when(active & jnp.logical_not(edge))
    def _inner_step():
        step(False)

    @pl.when(t == last)
    def _done():
        m_out[0] = to_row(m_sc[...])
        l_out[0] = to_row(l_sc[...])
        acc_out[0] = acc_sc[...]
        rows = q_ref.shape[0]
        own = rows // 2
        for j in range(GROUP):
            far_out[0, j] = acc_sc[j * rows + own:(j + 1) * rows].astype(far_out.dtype)


def attend(bounds, q, kv, halves, state=None):
    rows = q.shape[0]
    _, n_blocks, block_rows, _ = kv.shape
    tile_blocks = TILE_KEYS // block_rows
    n_tiles = n_blocks // tile_blocks
    qrows = rows * GROUP

    phases = len(halves)

    def half_of(t):
        return halves[0] if phases == 1 else t // n_tiles

    def tile_of(t, b):
        phase = t // n_tiles
        first = b[2 * phase] // tile_blocks + t % n_tiles
        return jnp.minimum(first, b[2 * phase + 1] // tile_blocks)

    in_specs = [
        pl.BlockSpec((rows, GROUP * HEAD_DIM), lambda g, t, b: (0, g)),
        pl.BlockSpec(
            (None, tile_blocks, block_rows, HEAD_DIM),
            lambda g, t, b: (half_of(t), tile_of(t, b), 0, g),
        ),
        pl.BlockSpec(
            (None, tile_blocks, block_rows, HEAD_DIM),
            lambda g, t, b: (half_of(t), tile_of(t, b), 0, KV_HEADS + g),
        ),
    ]
    operands = [q, kv, kv]
    state_specs = [
        pl.BlockSpec((1, 1, qrows), lambda g, t, b: (g, 0, 0)),
        pl.BlockSpec((1, 1, qrows), lambda g, t, b: (g, 0, 0)),
        pl.BlockSpec((1, qrows, HEAD_DIM), lambda g, t, b: (g, 0, 0)),
    ]
    state_shapes = [
        jax.ShapeDtypeStruct((KV_HEADS, 1, qrows), jnp.float32),
        jax.ShapeDtypeStruct((KV_HEADS, 1, qrows), jnp.float32),
        jax.ShapeDtypeStruct((KV_HEADS, qrows, HEAD_DIM), jnp.float32),
    ]
    out_specs = state_specs + [
        pl.BlockSpec((1, GROUP, rows // 2, HEAD_DIM), lambda g, t, b: (g, 0, 0, 0))
    ]
    out_shapes = state_shapes + [
        jax.ShapeDtypeStruct((KV_HEADS, GROUP, rows // 2, HEAD_DIM), jnp.bfloat16)
    ]
    if state is not None:
        in_specs += state_specs
        operands += list(state)
    kernel = functools.partial(
        attend_kernel, carry_in=state is not None, tiles_per_phase=n_tiles
    )
    tile_flops = 4 * qrows * TILE_KEYS * HEAD_DIM
    cost = pl.CostEstimate(
        flops=KV_HEADS * n_tiles * phases * tile_flops,
        transcendentals=KV_HEADS * n_tiles * phases * qrows * TILE_KEYS,
        bytes_accessed=kv.size + q.size * 2 + KV_HEADS * qrows * HEAD_DIM * 8,
    )
    return pl.pallas_call(
        kernel,
        grid_spec=pltpu.PrefetchScalarGridSpec(
            num_scalar_prefetch=1,
            grid=(KV_HEADS, n_tiles * phases),
            in_specs=in_specs,
            out_specs=out_specs,
            scratch_shapes=[
                pltpu.VMEM((qrows, HEAD_DIM), jnp.bfloat16),
                pltpu.VMEM((qrows, 1), jnp.float32),
                pltpu.VMEM((qrows, 1), jnp.float32),
                pltpu.VMEM((qrows, HEAD_DIM), jnp.float32),
                pltpu.VMEM((TILE_KEYS, 2 * HEAD_DIM), jnp.bfloat16),
            ],
        ),
        out_shape=out_shapes,
        compiler_params=pltpu.CompilerParams(
            dimension_semantics=("arbitrary", "arbitrary"),
        ),
        cost_estimate=cost,
    )(bounds, *operands)


def split_halves(state, own_rows):
    mine, theirs = [], []
    *state, far_acc = state
    for part in state:
        width = part.shape[-1] if part.shape[1] != 1 else 1
        shaped = part.reshape(KV_HEADS, GROUP, 2, own_rows, width)
        mine.append(shaped[:, :, 0])
        theirs.append(shaped[:, :, 1])
    theirs[-1] = far_acc
    return mine, theirs


def send_back(theirs, swap):
    run_max, run_sum, acc = theirs
    acc = lax.ppermute(acc.astype(jnp.bfloat16), "row", swap).astype(jnp.float32)
    stats = lax.ppermute(jnp.concatenate([run_max, run_sum], axis=-1), "row", swap)
    return [stats[..., 0:1], stats[..., 1:2], acc]


def finish(mine, theirs, gain):
    own_max, own_sum, own_acc = mine
    far_max, far_sum, far_acc = theirs
    top = jnp.maximum(own_max, far_max)
    own_factor = jnp.exp2((own_max - top) * EXP2_SCALE)
    far_factor = jnp.exp2((far_max - top) * EXP2_SCALE)
    total = own_sum * own_factor + far_sum * far_factor
    acc = own_acc * own_factor + far_acc * far_factor
    mixed = acc / total
    spread = jnp.sqrt(jnp.mean(mixed * mixed, axis=-1, keepdims=True) + 1e-06)
    normed = (mixed / spread * gain).astype(jnp.bfloat16)
    rows = normed.shape[2]
    return normed.transpose(2, 0, 1, 3).reshape(rows, KV_HEADS * GROUP * HEAD_DIM)


def per_device(queries, keys, values, gain, outer, inner):
    seq_index = lax.axis_index("outer") * inner + lax.axis_index("inner")
    last_index = outer * inner - 1
    own_rows = queries.shape[2]
    swap = [(0, 1), (1, 0)]
    partner_queries = lax.ppermute(queries, "row", swap)
    both_queries = jnp.concatenate([queries, partner_queries], axis=2)
    pair = jnp.concatenate([keys, values], axis=-1)
    blocks = lax.all_gather(pair[:, 0], "outer", axis=1, tiled=False)
    blocks = lax.all_gather(blocks, "inner", axis=2, tiled=False)
    blocks = blocks.reshape(2, outer * inner, own_rows, pair.shape[3])
    zero = jnp.int32(0)
    top = jnp.int32(last_index)

    early = attend(jnp.stack([zero, seq_index]), both_queries[0, 0], blocks, (0,))
    early_mine, early_theirs = split_halves(early, own_rows)

    late = attend(
        jnp.stack([zero, top, seq_index, top]), both_queries[1, 0], blocks, (0, 1)
    )
    late_mine, late_theirs = split_halves(late, own_rows)
    both_back = send_back([jnp.stack(pair) for pair in zip(early_theirs, late_theirs)], swap)
    early_back = [x[0] for x in both_back]
    late_back = [x[1] for x in both_back]

    early_out = finish(early_mine, early_back, gain)
    late_out = finish(late_mine, late_back, gain)
    return jnp.stack([early_out, late_out]).reshape(2, 1, own_rows, KV_HEADS * GROUP * HEAD_DIM)


def solution(mesh):
    seq_count, row_count = mesh.devices.shape
    outer = math.gcd(seq_count, 4)
    inner = seq_count // outer
    split = Mesh(mesh.devices.reshape(outer, inner, row_count), ("outer", "inner", "row"))
    spec = P(None, ("outer", "inner"), "row", None)
    return jax.shard_map(
        functools.partial(per_device, outer=outer, inner=inner),
        mesh=split,
        in_specs=(spec, spec, spec, P()),
        out_specs=spec,
        check_vma=False,
    )
```
